256 devices in a mesh: feat: 32 (over y, x, core), samp: 8 (over z).
Axes of the slice: x: 4, y: 4, z: 8, core: 2. Of those that a mesh axis runs over, the one named last changes fastest.
Arguments:
- hash_codes: int32 [32, 6144, 1024], P('feat', 'samp'), may hold values from 0 to 4095
- sample_index: int32 [32, 65536], P('feat', 'samp'), may hold values from 0 to 767, as said below
- labels: int32 [8192, 8], P('feat', 'samp'), may hold values 0 or 1
- encoder_first: bfloat16 [32, 1024, 2048], P('feat'), may hold values from -0.1875 to 0.1875
- encoder_second: bfloat16 [32, 2048, 256], P('feat'), may hold values from -0.125 to 0.125
- top_weight: bfloat16 [1024, 1024], replicated, may hold values from -0.1875 to 0.1875
- score_vector: bfloat16 [1024], replicated, may hold values from -0.1875 to 0.1875
Outputs:
- row_grads: float32 [32, 6144, 256], P('feat', 'samp')
- grad_first: float32 [32, 1024, 2048], P('feat', 'samp')
- grad_second: float32 [32, 2048, 256], P('feat', 'samp')
The draws below stay inside these ranges and needn't reach their ends.
Inputs may be any that keep to these rules, and one draw needn't show every extreme that they name: `sample_index`: for each feature and sample group the slots used by the group's 8192 samples are 0 to some count minus 1, each at least once; for some feature and group that count is 768.
All inputs are finite; a program needn't handle non-finite values. No bound on the sum of `labels` on one device may be relied on, other than what follows from the above.
Results may differ from the reference program's by a relative error of at most 0.019.
Values may be sent and summed in bfloat16 or wider, within the bound.
No kernel may reach another device: no remote copies, remote signals or barrier semaphores. Data moves between devices by JAX's collectives and lax.ppermute only.
A program may use at most 128 MiB of HBM per device.

```python
import jax
import jax.numpy as jnp
from jax import lax

HASHES = 1024
HID1 = 2048
EMB = 256
HID = 1024
BUCKETS = 4096
ROWS_DEV = 768
SB_DEV = 256
FEATS = 32
GROUPS = 8
GROUP = 8192
N_FEAT = 32
N_SAMP = 8


def draw_sample_index(key, part):
    group = SB_DEV * N_FEAT
    lanes = FEATS * N_SAMP
    key_count, key_pick, key_order, key_fill = jax.random.split(key, 4)
    counts = jax.random.randint(key_count, (lanes,), ROWS_DEV // 4, ROWS_DEV + 1)
    chosen = jax.random.randint(key_pick, (), 0, lanes)
    counts = jnp.where(jnp.arange(lanes) == chosen, ROWS_DEV, counts).astype(jnp.int32)
    scores = jax.random.randint(key_order, (lanes, group), 0, 2 ** 30 // group) * group + jnp.arange(group)[None, :]
    ordering = jnp.argsort(scores, axis=1).astype(jnp.int32)
    filler = jax.random.randint(key_fill, (lanes, group), 0, 2 ** 20)
    result = jnp.where(ordering < counts[:, None], ordering, filler % counts[:, None])
    return result.astype(jnp.int32).reshape(FEATS, N_SAMP * group)


def plant(entries, own_key, smallest, high):
    longest = entries.shape.index(max(entries.shape))
    spots = []
    for shift in (0, 1):
        where = [jax.random.randint(jax.random.fold_in(own_key, axis), (), 0, length) for axis, length in enumerate(entries.shape)]
        where[longest] = (where[longest] + shift) % entries.shape[longest]
        spots.append(tuple(where))
    return entries.at[spots[0]].set(smallest).at[spots[1]].set(high)


def block_levels(stream_key, shape, shards, least, largest):
    def one(axis_at, blocks):
        steps = jax.random.uniform(jax.random.fold_in(jax.random.fold_in(stream_key, 6), axis_at), (blocks,), jnp.float32, least / len(shards), largest / len(shards))
        return jnp.repeat(jnp.exp(steps), shape[axis_at] // blocks).reshape((-1,) + (1,) * (len(shape) - axis_at - 1))

    factor_of = one(*shards[0])
    for cut in shards[1:]:
        factor_of = factor_of * one(*cut)
    return factor_of


def bell_draw(own_key, extent, spread, reach, shards=(), kind=jnp.bfloat16):
    level = block_levels(own_key, extent, shards, -0.22, 0.18) if shards else 1.0
    values = jax.random.normal(own_key, extent, jnp.float32) * spread * level
    return jnp.minimum(jnp.maximum(values, -reach), reach).astype(kind)


def setup_inputs(seed: int = 0) -> dict:
    key_list = jax.random.split(jax.random.key(seed), 8)
    return {
        "hash_codes": plant(jax.random.randint(key_list[0], (FEATS, GROUPS * ROWS_DEV, HASHES), 0, BUCKETS), jax.random.fold_in(key_list[0], 1), 0, BUCKETS - 1).astype(jnp.int32),
        "sample_index": draw_sample_index(jax.random.fold_in(key_list[7], 71), 0),
        "labels": plant((jax.random.randint(key_list[2], (GROUP, GROUPS), 0, 2) < 1).astype(jnp.int32), jax.random.fold_in(key_list[2], 1), 0, 1),
        "encoder_first": bell_draw(key_list[3], (FEATS, HASHES, HID1), HASHES ** -0.5, 0.1875, ((0, 32),)),
        "encoder_second": bell_draw(key_list[4], (FEATS, HID1, EMB), HID1 ** -0.5, 0.125, ((0, 32),)),
        "top_weight": bell_draw(key_list[5], (FEATS * FEATS, HID), (FEATS * FEATS) ** -0.5, 0.1875),
        "score_vector": bell_draw(key_list[6], (HID,), HID ** -0.5, 0.1875),
    }


loss_scale = 256.0


def silu_slope(inputs):
    logistic = jax.nn.sigmoid(inputs)
    return logistic * (1.0 + inputs * (1.0 - logistic))


def encode_codes(codes_block):
    return (codes_block.astype(jnp.float32) * (2.0 / (BUCKETS - 1)) - 1.0).astype(jnp.bfloat16)


def take_rows(row_table, positions):
    return jnp.take(row_table, positions, axis=0)


def sum_rows(emb_delta, positions):
    return jax.ops.segment_sum(emb_delta.astype(jnp.float32), positions, num_segments=ROWS_DEV)


def top_tower(picked, label_block, top_weight, score_vector):
    feats, count, width = picked.shape
    picked_float = picked.astype(jnp.float32)
    weight_float = top_weight.astype(jnp.float32)
    pair_dots = (jnp.einsum("fne,hne->nfh", picked_float, picked_float) * (width ** -0.5)).astype(jnp.bfloat16)
    pair_flat = pair_dots.reshape(count, feats * feats)
    top_pre = jnp.dot(pair_flat, top_weight, preferred_element_type=jnp.float32)
    top_hidden = jax.nn.silu(top_pre).astype(jnp.bfloat16)
    logits = jnp.dot(top_hidden, score_vector, preferred_element_type=jnp.float32)
    dlogit = loss_scale * (jax.nn.sigmoid(logits) - label_block.astype(jnp.float32))
    top_delta = (dlogit[:, None] * score_vector.astype(jnp.float32)[None, :] * silu_slope(top_pre)).astype(jnp.bfloat16)
    pair_delta = jnp.einsum("nk,jk->nj", top_delta.astype(jnp.float32), weight_float).reshape(count, feats, feats)
    pair_sym = (pair_delta + jnp.swapaxes(pair_delta, 1, 2)).astype(jnp.bfloat16)
    emb_delta = jnp.einsum("nfh,hne->fne", pair_sym.astype(jnp.float32), picked_float) * (width ** -0.5)
    return emb_delta.astype(jnp.bfloat16)


def reference(hash_codes, sample_index, labels, encoder_first, encoder_second, top_weight, score_vector):
    group = SB_DEV * N_FEAT
    first_float = encoder_first.astype(jnp.float32)
    second_float = encoder_second.astype(jnp.float32)
    grad_first = jnp.zeros(encoder_first.shape, jnp.float32)
    grad_second = jnp.zeros(encoder_second.shape, jnp.float32)
    row_parts = []
    for group_id in range(N_SAMP):
        encoded = encode_codes(hash_codes[:, group_id * ROWS_DEV:(group_id + 1) * ROWS_DEV])
        encoded_float = encoded.astype(jnp.float32)
        first_pre = jnp.einsum("frh,fhk->frk", encoded_float, first_float)
        first_hidden = jax.nn.silu(first_pre).astype(jnp.bfloat16)
        row_table = jnp.einsum("frk,fke->fre", first_hidden.astype(jnp.float32), second_float).astype(jnp.bfloat16)
        positions = sample_index[:, group_id * group:(group_id + 1) * group]
        picked = jax.vmap(take_rows)(row_table, positions)
        emb_delta = top_tower(picked, labels[:, group_id], top_weight, score_vector)
        row_grads = jax.vmap(sum_rows)(emb_delta, positions)
        row_parts.append(row_grads)
        row_delta = row_grads.astype(jnp.bfloat16).astype(jnp.float32)
        second_term = jnp.einsum("frk,fre->fke", first_hidden.astype(jnp.float32), row_delta)
        first_delta = (jnp.einsum("fre,fke->frk", row_delta, second_float) * silu_slope(first_pre)).astype(jnp.bfloat16)
        first_term = jnp.einsum("frh,frk->fhk", encoded_float, first_delta.astype(jnp.float32))
        grad_second = grad_second + lax.optimization_barrier(second_term.astype(jnp.bfloat16)).astype(jnp.float32)
        grad_first = grad_first + lax.optimization_barrier(first_term.astype(jnp.bfloat16)).astype(jnp.float32)
    return jnp.concatenate(row_parts, axis=1), grad_first, grad_second
```

```python
import jax
import jax.numpy as jnp
from jax import lax
from jax.sharding import PartitionSpec as P

BUCKETS = 4096


loss_scale = 256.0


def silu_slope(inputs):
    logistic = jax.nn.sigmoid(inputs)
    return logistic * (1.0 + inputs * (1.0 - logistic))


def top_tower(picked, label_block, top_weight, score_vector):
    feats, count, width = picked.shape
    pair_dots = (
        jnp.einsum("fne,hne->nfh", picked, picked, preferred_element_type=jnp.float32)
        * width ** (-0.5)
    ).astype(jnp.bfloat16)
    pair_flat = pair_dots.reshape(count, feats * feats)
    top_pre = jnp.dot(pair_flat, top_weight, preferred_element_type=jnp.float32)
    top_hidden = jax.nn.silu(top_pre).astype(jnp.bfloat16)
    logits = jnp.dot(top_hidden, score_vector, preferred_element_type=jnp.float32)
    dlogit = loss_scale * (jax.nn.sigmoid(logits) - label_block.astype(jnp.float32))
    top_delta = (
        dlogit[:, None] * score_vector.astype(jnp.float32)[None, :] * silu_slope(top_pre)
    ).astype(jnp.bfloat16)
    pair_delta = jnp.einsum(
        "nk,jk->nj", top_delta, top_weight, preferred_element_type=jnp.float32
    ).reshape(count, feats, feats)
    pair_sym = (pair_delta + jnp.swapaxes(pair_delta, 1, 2)).astype(jnp.bfloat16)
    emb_delta = jnp.einsum(
        "nfh,hne->fne", pair_sym, picked, preferred_element_type=jnp.float32
    ) * width ** (-0.5)
    return emb_delta.astype(jnp.bfloat16)


def local(
    hash_codes, sample_index, labels, encoder_first, encoder_second, top_weight, score_vector
):
    feat_count = lax.axis_size("feat")
    encoded = (hash_codes[0].astype(jnp.float32) * (2.0 / (BUCKETS - 1)) - 1.0).astype(jnp.bfloat16)
    first_pre = jnp.dot(encoded, encoder_first[0], preferred_element_type=jnp.float32)
    first_hidden = jax.nn.silu(first_pre).astype(jnp.bfloat16)
    row_table = jnp.dot(first_hidden, encoder_second[0], preferred_element_type=jnp.float32).astype(
        jnp.bfloat16
    )
    positions = sample_index[0]
    slot_count = row_table.shape[0]
    emb_width = row_table.shape[1]
    select = (positions[:, None] == lax.broadcasted_iota(jnp.int32, (1, slot_count), 1)).astype(
        jnp.bfloat16
    )
    chosen_rows = (
        jnp.dot(select, row_table, preferred_element_type=jnp.float32)
        .astype(jnp.bfloat16)
        .reshape(feat_count, -1, emb_width)
    )
    picked = lax.all_to_all(chosen_rows, "feat", split_axis=0, concat_axis=0, tiled=True)
    emb_delta = top_tower(picked, labels[:, 0], top_weight, score_vector)
    returned = lax.all_to_all(emb_delta, "feat", split_axis=0, concat_axis=0, tiled=True)
    row_grads = jnp.einsum(
        "nu,ne->ue", select, returned.reshape(-1, emb_width), preferred_element_type=jnp.float32
    )
    row_delta = row_grads.astype(jnp.bfloat16)
    second_local = jnp.einsum(
        "rk,re->ke", first_hidden, row_delta, preferred_element_type=jnp.float32
    )
    first_back = jnp.einsum(
        "re,ke->rk", row_delta, encoder_second[0], preferred_element_type=jnp.float32
    )
    first_delta = (first_back * silu_slope(first_pre)).astype(jnp.bfloat16)
    first_local = jnp.einsum("rh,rk->hk", encoded, first_delta, preferred_element_type=jnp.float32)
    share_first = lax.psum_scatter(
        first_local.astype(jnp.bfloat16), "samp", scatter_dimension=0, tiled=True
    ).astype(jnp.float32)
    share_second = lax.psum_scatter(
        second_local.astype(jnp.bfloat16), "samp", scatter_dimension=0, tiled=True
    ).astype(jnp.float32)
    return (row_grads[None], share_first[None], share_second[None])


def solution(mesh):
    return jax.shard_map(
        local,
        mesh=mesh,
        in_specs=(
            P("feat", "samp", None),
            P("feat", "samp"),
            P("feat", "samp"),
            P("feat", None, None),
            P("feat", None, None),
            P(),
            P(),
        ),
        out_specs=(P("feat", "samp", None), P("feat", "samp", None), P("feat", "samp", None)),
        check_vma=False,
    )
```

```python
import jax
import jax.numpy as jnp
from jax import lax
from jax.sharding import PartitionSpec as P

BUCKETS = 4096


loss_scale = 256.0


def silu_slope(inputs):
    logistic = jax.nn.sigmoid(inputs)
    return logistic * (1.0 + inputs * (1.0 - logistic))


def top_tower(picked, label_block, top_weight, score_vector):
    feats, count, width = picked.shape
    pair_dots = (
        jnp.einsum("fne,hne->nfh", picked, picked, preferred_element_type=jnp.float32)
        * width ** (-0.5)
    ).astype(jnp.bfloat16)
    pair_flat = pair_dots.reshape(count, feats * feats)
    top_pre = jnp.dot(pair_flat, top_weight, preferred_element_type=jnp.float32)
    top_hidden = jax.nn.silu(top_pre).astype(jnp.bfloat16)
    logits = jnp.dot(top_hidden, score_vector, preferred_element_type=jnp.float32)
    dlogit = loss_scale * (jax.nn.sigmoid(logits) - label_block.astype(jnp.float32))
    top_delta = (
        dlogit[:, None] * score_vector.astype(jnp.float32)[None, :] * silu_slope(top_pre)
    ).astype(jnp.bfloat16)
    pair_delta = jnp.einsum(
        "nk,jk->nj", top_delta, top_weight, preferred_element_type=jnp.float32
    ).reshape(count, feats, feats)
    pair_sym = (pair_delta + jnp.swapaxes(pair_delta, 1, 2)).astype(jnp.bfloat16)
    emb_delta = jnp.einsum(
        "nfh,hne->fne", pair_sym, picked, preferred_element_type=jnp.float32
    ) * width ** (-0.5)
    return emb_delta.astype(jnp.bfloat16)


def local(
    hash_codes, sample_index, labels, encoder_first, encoder_second, top_weight, score_vector
):
    feat_count = lax.axis_size("feat")
    encoded = (hash_codes[0].astype(jnp.float32) * (2.0 / (BUCKETS - 1)) - 1.0).astype(jnp.bfloat16)
    first_pre = jnp.dot(encoded, encoder_first[0], preferred_element_type=jnp.float32)
    first_hidden = jax.nn.silu(first_pre).astype(jnp.bfloat16)
    row_table = jnp.dot(first_hidden, encoder_second[0], preferred_element_type=jnp.float32).astype(
        jnp.bfloat16
    )
    positions = sample_index[0]
    slot_count = row_table.shape[0]
    emb_width = row_table.shape[1]
    select = (positions[:, None] == lax.broadcasted_iota(jnp.int32, (1, slot_count), 1)).astype(
        jnp.bfloat16
    )
    chosen_rows = (
        jnp.dot(select, row_table, preferred_element_type=jnp.float32)
        .astype(jnp.bfloat16)
        .reshape(feat_count, -1, emb_width)
    )
    picked = lax.all_to_all(chosen_rows, "feat", split_axis=0, concat_axis=0, tiled=True)
    emb_delta = top_tower(picked, labels[:, 0], top_weight, score_vector)
    returned = lax.all_to_all(emb_delta, "feat", split_axis=0, concat_axis=0, tiled=True)
    row_grads = jnp.einsum(
        "nu,ne->ue", select, returned.reshape(-1, emb_width), preferred_element_type=jnp.float32
    )
    row_delta = row_grads.astype(jnp.bfloat16)
    second_local = jnp.einsum(
        "rk,re->ke", first_hidden, row_delta, preferred_element_type=jnp.float32
    )
    first_back = jnp.einsum(
        "re,ke->rk", row_delta, encoder_second[0], preferred_element_type=jnp.float32
    )
    first_delta = (first_back * silu_slope(first_pre)).astype(jnp.bfloat16)
    first_local = jnp.einsum("rh,rk->hk", encoded, first_delta, preferred_element_type=jnp.float32)
    group_count = lax.axis_size("samp")
    first_rows = first_local.shape[0] // group_count
    second_rows = second_local.shape[0] // group_count
    hid_width = first_local.shape[1]
    merged = jnp.concatenate(
        [
            first_local.astype(jnp.bfloat16).reshape(group_count, first_rows, hid_width),
            second_local.astype(jnp.bfloat16).reshape(group_count, -1, hid_width),
        ],
        axis=1,
    ).reshape(-1, hid_width)
    share = lax.psum_scatter(merged, "samp", scatter_dimension=0, tiled=True).astype(jnp.float32)
    share_first = share[:first_rows]
    share_second = share[first_rows:].reshape(second_rows, emb_width)
    return (row_grads[None], share_first[None], share_second[None])


def solution(mesh):
    return jax.shard_map(
        local,
        mesh=mesh,
        in_specs=(
            P("feat", "samp", None),
            P("feat", "samp"),
            P("feat", "samp"),
            P("feat", None, None),
            P("feat", None, None),
            P(),
            P(),
        ),
        out_specs=(P("feat", "samp", None), P("feat", "samp", None), P("feat", "samp", None)),
        check_vma=False,
    )
```

```python
import jax
import jax.numpy as jnp
from jax import lax
from jax.sharding import PartitionSpec as P

BUCKETS = 4096


loss_scale = 256.0


def silu_slope(inputs):
    logistic = jax.nn.sigmoid(inputs)
    return logistic * (1.0 + inputs * (1.0 - logistic))


def top_tower(picked, label_block, top_weight, score_vector):
    feats, count, width = picked.shape
    pair_dots = (
        jnp.einsum("fne,hne->nfh", picked, picked, preferred_element_type=jnp.float32)
        * width ** (-0.5)
    ).astype(jnp.bfloat16)
    pair_flat = pair_dots.reshape(count, feats * feats)
    top_pre = jnp.dot(pair_flat, top_weight, preferred_element_type=jnp.float32)
    top_hidden = jax.nn.silu(top_pre).astype(jnp.bfloat16)
    logits = jnp.dot(top_hidden, score_vector, preferred_element_type=jnp.float32)
    dlogit = loss_scale * (jax.nn.sigmoid(logits) - label_block.astype(jnp.float32))
    top_delta = (
        dlogit[:, None] * score_vector.astype(jnp.float32)[None, :] * silu_slope(top_pre)
    ).astype(jnp.bfloat16)
    pair_delta = jnp.einsum(
        "nk,jk->nj", top_delta, top_weight, preferred_element_type=jnp.float32
    ).reshape(count, feats, feats)
    pair_sym = (pair_delta + jnp.swapaxes(pair_delta, 1, 2)).astype(jnp.bfloat16)
    emb_delta = jnp.einsum(
        "nfh,hne->fne", pair_sym, picked, preferred_element_type=jnp.float32
    ) * width ** (-0.5)
    return emb_delta.astype(jnp.bfloat16)


def local(
    hash_codes, sample_index, labels, encoder_first, encoder_second, top_weight, score_vector
):
    feat_count = lax.axis_size("feat")
    encoded = (hash_codes[0].astype(jnp.float32) * (2.0 / (BUCKETS - 1)) - 1.0).astype(jnp.bfloat16)
    first_pre = jnp.dot(encoded, encoder_first[0], preferred_element_type=jnp.float32)
    first_hidden = jax.nn.silu(first_pre).astype(jnp.bfloat16)
    row_table = jnp.dot(first_hidden, encoder_second[0], preferred_element_type=jnp.float32).astype(
        jnp.bfloat16
    )
    positions = sample_index[0]
    slot_count = row_table.shape[0]
    emb_width = row_table.shape[1]
    chunk_count = 2
    per_dest = positions.shape[0] // feat_count
    chunk_len = per_dest // chunk_count
    slot_iota = lax.broadcasted_iota(jnp.int32, (1, slot_count), 1)
    label_column = labels[:, 0]
    grad_parts = []
    for chunk in range(chunk_count):
        chunk_positions = positions.reshape(feat_count, per_dest)[
            :, chunk * chunk_len : (chunk + 1) * chunk_len
        ].reshape(-1)
        select = (chunk_positions[:, None] == slot_iota).astype(jnp.bfloat16)
        chosen_rows = (
            jnp.dot(select, row_table, preferred_element_type=jnp.float32)
            .astype(jnp.bfloat16)
            .reshape(feat_count, chunk_len, emb_width)
        )
        picked = lax.all_to_all(chosen_rows, "feat", split_axis=0, concat_axis=0, tiled=True)
        emb_delta = top_tower(
            picked,
            label_column[chunk * chunk_len : (chunk + 1) * chunk_len],
            top_weight,
            score_vector,
        )
        returned = lax.all_to_all(emb_delta, "feat", split_axis=0, concat_axis=0, tiled=True)
        grad_parts.append(
            jnp.einsum(
                "nu,ne->ue",
                select,
                returned.reshape(-1, emb_width),
                preferred_element_type=jnp.float32,
            )
        )
    row_grads = grad_parts[0]
    for part in grad_parts[1:]:
        row_grads = row_grads + part
    row_delta = row_grads.astype(jnp.bfloat16)
    second_local = jnp.einsum(
        "rk,re->ke", first_hidden, row_delta, preferred_element_type=jnp.float32
    )
    first_back = jnp.einsum(
        "re,ke->rk", row_delta, encoder_second[0], preferred_element_type=jnp.float32
    )
    first_delta = (first_back * silu_slope(first_pre)).astype(jnp.bfloat16)
    first_local = jnp.einsum("rh,rk->hk", encoded, first_delta, preferred_element_type=jnp.float32)
    group_count = lax.axis_size("samp")
    first_rows = first_local.shape[0] // group_count
    second_rows = second_local.shape[0] // group_count
    hid_width = first_local.shape[1]
    merged = jnp.concatenate(
        [
            first_local.astype(jnp.bfloat16).reshape(group_count, first_rows, hid_width),
            second_local.astype(jnp.bfloat16).reshape(group_count, -1, hid_width),
        ],
        axis=1,
    ).reshape(-1, hid_width)
    share = lax.psum_scatter(merged, "samp", scatter_dimension=0, tiled=True).astype(jnp.float32)
    share_first = share[:first_rows]
    share_second = share[first_rows:].reshape(second_rows, emb_width)
    return (row_grads[None], share_first[None], share_second[None])


def solution(mesh):
    return jax.shard_map(
        local,
        mesh=mesh,
        in_specs=(
            P("feat", "samp", None),
            P("feat", "samp"),
            P("feat", "samp"),
            P("feat", None, None),
            P("feat", None, None),
            P(),
            P(),
        ),
        out_specs=(P("feat", "samp", None), P("feat", "samp", None), P("feat", "samp", None)),
        check_vma=False,
    )
```

```python
import jax
import jax.numpy as jnp
from jax import lax
from jax.sharding import PartitionSpec as P

BUCKETS = 4096


loss_scale = 256.0


def silu_slope(inputs):
    logistic = jax.nn.sigmoid(inputs)
    return logistic * (1.0 + inputs * (1.0 - logistic))


def top_tower(picked, label_block, top_weight, score_vector):
    feats, count, width = picked.shape
    pair_dots = (
        jnp.einsum("fne,hne->nfh", picked, picked, preferred_element_type=jnp.float32)
        * width ** (-0.5)
    ).astype(jnp.bfloat16)
    pair_flat = pair_dots.reshape(count, feats * feats)
    top_pre = jnp.dot(pair_flat, top_weight, preferred_element_type=jnp.float32)
    top_hidden = jax.nn.silu(top_pre).astype(jnp.bfloat16)
    logits = jnp.dot(top_hidden, score_vector, preferred_element_type=jnp.float32)
    dlogit = loss_scale * (jax.nn.sigmoid(logits) - label_block.astype(jnp.float32))
    top_delta = (
        dlogit[:, None] * score_vector.astype(jnp.float32)[None, :] * silu_slope(top_pre)
    ).astype(jnp.bfloat16)
    pair_delta = jnp.einsum(
        "nk,jk->nj", top_delta, top_weight, preferred_element_type=jnp.float32
    ).reshape(count, feats, feats)
    pair_sym = (pair_delta + jnp.swapaxes(pair_delta, 1, 2)).astype(jnp.bfloat16)
    emb_delta = jnp.einsum(
        "nfh,hne->fne", pair_sym, picked, preferred_element_type=jnp.float32
    ) * width ** (-0.5)
    return emb_delta.astype(jnp.bfloat16)


def local(
    hash_codes, sample_index, labels, encoder_first, encoder_second, top_weight, score_vector
):
    feat_count = lax.axis_size("feat")
    encoded = (hash_codes[0].astype(jnp.float32) * (2.0 / (BUCKETS - 1)) - 1.0).astype(jnp.bfloat16)
    first_pre = jnp.dot(encoded, encoder_first[0], preferred_element_type=jnp.float32)
    first_hidden = jax.nn.silu(first_pre).astype(jnp.bfloat16)
    row_table = jnp.dot(first_hidden, encoder_second[0], preferred_element_type=jnp.float32).astype(
        jnp.bfloat16
    )
    positions = sample_index[0]
    slot_count = row_table.shape[0]
    emb_width = row_table.shape[1]
    chunk_count = 2
    per_dest = positions.shape[0] // feat_count
    chunk_len = per_dest // chunk_count
    slot_iota = lax.broadcasted_iota(jnp.int32, (1, slot_count), 1)
    label_column = labels[:, 0]
    grad_parts = []
    for chunk in range(chunk_count):
        chunk_positions = positions.reshape(feat_count, per_dest)[
            :, chunk * chunk_len : (chunk + 1) * chunk_len
        ].reshape(-1)
        select = (chunk_positions[:, None] == slot_iota).astype(jnp.bfloat16)
        chosen_rows = (
            jnp.dot(select, row_table, preferred_element_type=jnp.float32)
            .astype(jnp.bfloat16)
            .reshape(feat_count, chunk_len, emb_width)
        )
        picked = lax.all_to_all(chosen_rows, "feat", split_axis=0, concat_axis=0, tiled=True)
        emb_delta = top_tower(
            picked,
            label_column[chunk * chunk_len : (chunk + 1) * chunk_len],
            top_weight,
            score_vector,
        )
        returned = lax.all_to_all(emb_delta, "feat", split_axis=0, concat_axis=0, tiled=True)
        grad_parts.append(
            jnp.einsum(
                "nu,ne->ue",
                select,
                returned.reshape(-1, emb_width),
                preferred_element_type=jnp.float32,
            )
        )
    row_grads = grad_parts[0]
    for part in grad_parts[1:]:
        row_grads = row_grads + part
    row_delta = row_grads.astype(jnp.bfloat16)
    second_local = jnp.einsum(
        "rk,re->ke", first_hidden, row_delta, preferred_element_type=jnp.float32
    )
    first_back = jnp.einsum(
        "re,ke->rk", row_delta, encoder_second[0], preferred_element_type=jnp.float32
    )
    first_delta = (first_back * silu_slope(first_pre)).astype(jnp.bfloat16)
    group_count = lax.axis_size("samp")
    shard_id = lax.axis_index("samp")
    hid_width = first_delta.shape[1]
    half_width = hid_width // 2
    first_rows = encoded.shape[1] // group_count
    second_rows = second_local.shape[0] // group_count
    second_split = second_local.astype(jnp.bfloat16).astype(jnp.float32).reshape(
        group_count, 2, second_rows // 2, emb_width
    )
    pieces = []
    for side in range(2):
        first_half = jnp.einsum(
            "rh,rk->hk",
            encoded,
            first_delta[:, side * half_width : (side + 1) * half_width],
            preferred_element_type=jnp.float32,
        )
        first_half = first_half.astype(jnp.bfloat16).astype(jnp.float32)
        pieces.append(
            jnp.concatenate(
                [first_half.reshape(group_count, first_rows, half_width), second_split[:, side]],
                axis=2,
            )
        )
    results = []
    for side, step in ((0, 1), (1, -1)):
        piece = pieces[side]
        ring = [(j, (j + step) % group_count) for j in range(group_count)]
        acc = lax.dynamic_index_in_dim(piece, (shard_id - step) % group_count, 0, keepdims=False)
        for hop in range(group_count - 1):
            recv = lax.ppermute(acc.astype(jnp.bfloat16), "samp", ring)
            block = (shard_id - step * (hop + 2)) % group_count
            acc = recv.astype(jnp.float32) + lax.dynamic_index_in_dim(
                piece, block, 0, keepdims=False
            )
        results.append(acc)
    share_first = jnp.concatenate([part[:, :half_width] for part in results], axis=1)
    share_second = jnp.concatenate([part[:, half_width:] for part in results], axis=0)
    return (row_grads[None], share_first[None], share_second[None])


def solution(mesh):
    return jax.shard_map(
        local,
        mesh=mesh,
        in_specs=(
            P("feat", "samp", None),
            P("feat", "samp"),
            P("feat", "samp"),
            P("feat", None, None),
            P("feat", None, None),
            P(),
            P(),
        ),
        out_specs=(P("feat", "samp", None), P("feat", "samp", None), P("feat", "samp", None)),
        check_vma=False,
    )
```

```python
import jax
import jax.numpy as jnp
from jax import lax
from jax.sharding import PartitionSpec as P

BUCKETS = 4096


loss_scale = 256.0


def silu_slope(inputs):
    logistic = jax.nn.sigmoid(inputs)
    return logistic * (1.0 + inputs * (1.0 - logistic))


def top_tower(picked, label_block, top_weight, score_vector):
    feats, count, width = picked.shape
    pair_dots = (
        jnp.einsum("fne,hne->nfh", picked, picked, preferred_element_type=jnp.float32)
        * width ** (-0.5)
    ).astype(jnp.bfloat16)
    pair_flat = pair_dots.reshape(count, feats * feats)
    top_pre = jnp.dot(pair_flat, top_weight, preferred_element_type=jnp.float32)
    top_hidden = jax.nn.silu(top_pre).astype(jnp.bfloat16)
    logits = jnp.dot(top_hidden, score_vector, preferred_element_type=jnp.float32)
    dlogit = loss_scale * (jax.nn.sigmoid(logits) - label_block.astype(jnp.float32))
    top_delta = (
        dlogit[:, None] * score_vector.astype(jnp.float32)[None, :] * silu_slope(top_pre)
    ).astype(jnp.bfloat16)
    pair_delta = jnp.einsum(
        "nk,jk->nj", top_delta, top_weight, preferred_element_type=jnp.float32
    ).reshape(count, feats, feats)
    pair_sym = (pair_delta + jnp.swapaxes(pair_delta, 1, 2)).astype(jnp.bfloat16)
    emb_delta = jnp.einsum(
        "nfh,hne->fne", pair_sym, picked, preferred_element_type=jnp.float32
    ) * width ** (-0.5)
    return emb_delta.astype(jnp.bfloat16)


def local(
    hash_codes, sample_index, labels, encoder_first, encoder_second, top_weight, score_vector
):
    feat_count = lax.axis_size("feat")
    encoded = (hash_codes[0].astype(jnp.float32) * (2.0 / (BUCKETS - 1)) - 1.0).astype(jnp.bfloat16)
    first_pre = jnp.dot(encoded, encoder_first[0], preferred_element_type=jnp.float32)
    first_hidden = jax.nn.silu(first_pre).astype(jnp.bfloat16)
    row_table = jnp.dot(first_hidden, encoder_second[0], preferred_element_type=jnp.float32).astype(
        jnp.bfloat16
    )
    positions = sample_index[0]
    slot_count = row_table.shape[0]
    emb_width = row_table.shape[1]
    chunk_count = 2
    per_dest = positions.shape[0] // feat_count
    chunk_len = per_dest // chunk_count
    slot_iota = lax.broadcasted_iota(jnp.int32, (1, slot_count), 1)
    label_column = labels[:, 0]
    grad_parts = []
    for chunk in range(chunk_count):
        chunk_positions = positions.reshape(feat_count, per_dest)[
            :, chunk * chunk_len : (chunk + 1) * chunk_len
        ].reshape(-1)
        select = (chunk_positions[:, None] == slot_iota).astype(jnp.bfloat16)
        chosen_rows = (
            jnp.dot(select, row_table, preferred_element_type=jnp.float32)
            .astype(jnp.bfloat16)
            .reshape(feat_count, chunk_len, emb_width)
        )
        picked = lax.all_to_all(chosen_rows, "feat", split_axis=0, concat_axis=0, tiled=True)
        emb_delta = top_tower(
            picked,
            label_column[chunk * chunk_len : (chunk + 1) * chunk_len],
            top_weight,
            score_vector,
        )
        returned = lax.all_to_all(emb_delta, "feat", split_axis=0, concat_axis=0, tiled=True)
        grad_parts.append(
            jnp.einsum(
                "nu,ne->ue",
                select,
                returned.reshape(-1, emb_width),
                preferred_element_type=jnp.float32,
            )
        )
    row_grads = grad_parts[0]
    for part in grad_parts[1:]:
        row_grads = row_grads + part
    row_delta = row_grads.astype(jnp.bfloat16)
    second_local = jnp.einsum(
        "rk,re->ke", first_hidden, row_delta, preferred_element_type=jnp.float32
    )
    first_back = jnp.einsum(
        "re,ke->rk", row_delta, encoder_second[0], preferred_element_type=jnp.float32
    )
    first_delta = (first_back * silu_slope(first_pre)).astype(jnp.bfloat16)
    group_count = lax.axis_size("samp")
    shard_id = lax.axis_index("samp")
    hid_width = first_delta.shape[1]
    half_width = hid_width // 2
    first_rows = encoded.shape[1] // group_count
    second_rows = second_local.shape[0] // group_count
    second_split = second_local.astype(jnp.bfloat16).astype(jnp.float32).reshape(
        group_count, 2, second_rows // 2, emb_width
    )
    pieces = []
    for side in range(2):
        first_half = jnp.einsum(
            "rh,rk->hk",
            encoded,
            first_delta[:, side * half_width : (side + 1) * half_width],
            preferred_element_type=jnp.float32,
        )
        first_half = first_half.astype(jnp.bfloat16).astype(jnp.float32)
        pieces.append(
            jnp.concatenate(
                [first_half.reshape(group_count, first_rows, half_width), second_split[:, side]],
                axis=2,
            )
        )
    chains = []
    for side, step in ((0, 1), (1, -1)):
        piece_rows = pieces[side].shape[1] // 2
        for part in range(2):
            piece = pieces[side][:, part * piece_rows : (part + 1) * piece_rows]
            acc = lax.dynamic_index_in_dim(
                piece, (shard_id - step) % group_count, 0, keepdims=False
            )
            chains.append([piece, step, acc])
    for hop in range(group_count - 1):
        for chain in chains:
            piece, step, acc = chain
            ring = [(j, (j + step) % group_count) for j in range(group_count)]
            recv = lax.ppermute(acc.astype(jnp.bfloat16), "samp", ring)
            block = (shard_id - step * (hop + 2)) % group_count
            chain[2] = recv.astype(jnp.float32) + lax.dynamic_index_in_dim(
                piece, block, 0, keepdims=False
            )
    results = [
        jnp.concatenate([chains[0][2], chains[1][2]], axis=0),
        jnp.concatenate([chains[2][2], chains[3][2]], axis=0),
    ]
    share_first = jnp.concatenate([part[:, :half_width] for part in results], axis=1)
    share_second = jnp.concatenate([part[:, half_width:] for part in results], axis=0)
    return (row_grads[None], share_first[None], share_second[None])


def solution(mesh):
    return jax.shard_map(
        local,
        mesh=mesh,
        in_specs=(
            P("feat", "samp", None),
            P("feat", "samp"),
            P("feat", "samp"),
            P("feat", None, None),
            P("feat", None, None),
            P(),
            P(),
        ),
        out_specs=(P("feat", "samp", None), P("feat", "samp", None), P("feat", "samp", None)),
        check_vma=False,
    )
```

```python
import jax
import jax.numpy as jnp
from jax import lax
from jax.sharding import PartitionSpec as P

BUCKETS = 4096


loss_scale = 256.0


def silu_slope(inputs):
    logistic = jax.nn.sigmoid(inputs)
    return logistic * (1.0 + inputs * (1.0 - logistic))


def top_tower(picked, label_block, top_weight, score_vector):
    feats, count, width = picked.shape
    pair_dots = (
        jnp.einsum("fne,hne->nfh", picked, picked, preferred_element_type=jnp.float32)
        * width ** (-0.5)
    ).astype(jnp.bfloat16)
    pair_flat = pair_dots.reshape(count, feats * feats)
    top_pre = jnp.dot(pair_flat, top_weight, preferred_element_type=jnp.float32)
    top_hidden = jax.nn.silu(top_pre).astype(jnp.bfloat16)
    logits = jnp.dot(top_hidden, score_vector, preferred_element_type=jnp.float32)
    dlogit = loss_scale * (jax.nn.sigmoid(logits) - label_block.astype(jnp.float32))
    top_delta = (
        dlogit[:, None] * score_vector.astype(jnp.float32)[None, :] * silu_slope(top_pre)
    ).astype(jnp.bfloat16)
    pair_delta = jnp.einsum(
        "nk,jk->nj", top_delta, top_weight, preferred_element_type=jnp.float32
    ).reshape(count, feats, feats)
    pair_sym = (pair_delta + jnp.swapaxes(pair_delta, 1, 2)).astype(jnp.bfloat16)
    emb_delta = jnp.einsum(
        "nfh,hne->fne", pair_sym, picked, preferred_element_type=jnp.float32
    ) * width ** (-0.5)
    return emb_delta.astype(jnp.bfloat16)


def local(
    hash_codes, sample_index, labels, encoder_first, encoder_second, top_weight, score_vector
):
    feat_count = lax.axis_size("feat")
    encoded = (hash_codes[0].astype(jnp.float32) * (2.0 / (BUCKETS - 1)) - 1.0).astype(jnp.bfloat16)
    first_pre = jnp.dot(encoded, encoder_first[0], preferred_element_type=jnp.float32)
    first_hidden = jax.nn.silu(first_pre).astype(jnp.bfloat16)
    row_table = jnp.dot(first_hidden, encoder_second[0], preferred_element_type=jnp.float32).astype(
        jnp.bfloat16
    )
    positions = sample_index[0]
    slot_count = row_table.shape[0]
    emb_width = row_table.shape[1]
    chunk_count = 2
    per_dest = positions.shape[0] // feat_count
    chunk_len = per_dest // chunk_count
    slot_iota = lax.broadcasted_iota(jnp.int32, (1, slot_count), 1)
    label_column = labels[:, 0]
    grad_parts = []
    for chunk in range(chunk_count):
        chunk_positions = positions.reshape(feat_count, per_dest)[
            :, chunk * chunk_len : (chunk + 1) * chunk_len
        ].reshape(-1)
        select = (chunk_positions[:, None] == slot_iota).astype(jnp.bfloat16)
        chosen_rows = (
            jnp.dot(select, row_table, preferred_element_type=jnp.float32)
            .astype(jnp.bfloat16)
            .reshape(feat_count, chunk_len, emb_width)
        )
        picked = lax.all_to_all(chosen_rows, "feat", split_axis=0, concat_axis=0, tiled=True)
        emb_delta = top_tower(
            picked,
            label_column[chunk * chunk_len : (chunk + 1) * chunk_len],
            top_weight,
            score_vector,
        )
        returned = lax.all_to_all(emb_delta, "feat", split_axis=0, concat_axis=0, tiled=True)
        grad_parts.append(
            jnp.einsum(
                "nu,ne->ue",
                select,
                returned.reshape(-1, emb_width),
                preferred_element_type=jnp.float32,
            )
        )
    row_grads = grad_parts[0]
    for part in grad_parts[1:]:
        row_grads = row_grads + part
    row_delta = row_grads.astype(jnp.bfloat16)
    second_local = jnp.einsum(
        "rk,re->ke", first_hidden, row_delta, preferred_element_type=jnp.float32
    )
    first_back = jnp.einsum(
        "re,ke->rk", row_delta, encoder_second[0], preferred_element_type=jnp.float32
    )
    first_delta = (first_back * silu_slope(first_pre)).astype(jnp.bfloat16)
    group_count = lax.axis_size("samp")
    shard_id = lax.axis_index("samp")
    hid_width = first_delta.shape[1]
    half_width = hid_width // 2
    first_rows = encoded.shape[1] // group_count
    second_rows = second_local.shape[0] // group_count
    second_split = second_local.astype(jnp.bfloat16).astype(jnp.float32).reshape(
        group_count, 2, second_rows // 2, emb_width
    )
    pieces = []
    for side in range(2):
        first_half = jnp.einsum(
            "rh,rk->hk",
            encoded,
            first_delta[:, side * half_width : (side + 1) * half_width],
            preferred_element_type=jnp.float32,
        )
        first_half = first_half.astype(jnp.bfloat16).astype(jnp.float32)
        pieces.append(
            jnp.concatenate(
                [first_half.reshape(group_count, first_rows, half_width), second_split[:, side]],
                axis=2,
            )
        )
    chains = []
    for side, step in ((0, 1), (1, -1)):
        piece_rows = pieces[side].shape[1] // 2
        for part in range(2):
            piece = pieces[side][:, part * piece_rows : (part + 1) * piece_rows]
            acc = lax.dynamic_index_in_dim(
                piece, (shard_id - step) % group_count, 0, keepdims=False
            )
            chains.append([piece, step, acc])
    def ring_hop(hop, accs):
        new_accs = []
        for (piece, step, _), acc in zip(chains, accs):
            ring = [(j, (j + step) % group_count) for j in range(group_count)]
            recv = lax.ppermute(acc.astype(jnp.bfloat16), "samp", ring)
            block = (shard_id - step * (hop + 2)) % group_count
            new_accs.append(
                recv.astype(jnp.float32)
                + lax.dynamic_index_in_dim(piece, block, 0, keepdims=False)
            )
        return tuple(new_accs)

    final_accs = lax.fori_loop(
        0, group_count - 1, ring_hop, tuple(chain[2] for chain in chains)
    )
    for chain, acc in zip(chains, final_accs):
        chain[2] = acc
    results = [
        jnp.concatenate([chains[0][2], chains[1][2]], axis=0),
        jnp.concatenate([chains[2][2], chains[3][2]], axis=0),
    ]
    share_first = jnp.concatenate([part[:, :half_width] for part in results], axis=1)
    share_second = jnp.concatenate([part[:, half_width:] for part in results], axis=0)
    return (row_grads[None], share_first[None], share_second[None])


def solution(mesh):
    return jax.shard_map(
        local,
        mesh=mesh,
        in_specs=(
            P("feat", "samp", None),
            P("feat", "samp"),
            P("feat", "samp"),
            P("feat", None, None),
            P("feat", None, None),
            P(),
            P(),
        ),
        out_specs=(P("feat", "samp", None), P("feat", "samp", None), P("feat", "samp", None)),
        check_vma=False,
    )
```

```python
import jax
import jax.numpy as jnp
from jax import lax
from jax.sharding import PartitionSpec as P

BUCKETS = 4096


loss_scale = 256.0


def silu_slope(inputs):
    logistic = jax.nn.sigmoid(inputs)
    return logistic * (1.0 + inputs * (1.0 - logistic))


def top_tower(picked, label_block, top_weight, score_vector):
    count, feats, width = picked.shape
    group = 8
    blocks = count // group
    side = group * feats
    grouped = picked.reshape(blocks, side, width)
    diagonal = (
        lax.broadcasted_iota(jnp.int32, (group, 1, group, 1), 0)
        == lax.broadcasted_iota(jnp.int32, (group, 1, group, 1), 2)
    )
    gram = jnp.einsum("gie,gje->gij", grouped, grouped, preferred_element_type=jnp.float32)
    gram = gram.reshape(blocks, group, feats, group, feats)
    pair_raw = jnp.sum(jnp.where(diagonal[None], gram, 0.0), axis=3)
    pair_dots = (pair_raw * width ** (-0.5)).astype(jnp.bfloat16)
    pair_flat = pair_dots.reshape(count, feats * feats)
    top_pre = jnp.dot(pair_flat, top_weight, preferred_element_type=jnp.float32)
    top_hidden = jax.nn.silu(top_pre).astype(jnp.bfloat16)
    logits = jnp.dot(top_hidden, score_vector, preferred_element_type=jnp.float32)
    dlogit = loss_scale * (jax.nn.sigmoid(logits) - label_block.astype(jnp.float32))
    top_delta = (
        dlogit[:, None] * score_vector.astype(jnp.float32)[None, :] * silu_slope(top_pre)
    ).astype(jnp.bfloat16)
    pair_delta = jnp.einsum(
        "nk,jk->nj", top_delta, top_weight, preferred_element_type=jnp.float32
    ).reshape(count, feats, feats)
    pair_sym = (pair_delta + jnp.swapaxes(pair_delta, 1, 2)).astype(jnp.bfloat16)
    sym_blocks = pair_sym.reshape(blocks, group, feats, 1, feats)
    block_diag = jnp.where(diagonal[None], sym_blocks, jnp.zeros((), jnp.bfloat16))
    block_diag = block_diag.reshape(blocks, side, side)
    emb_delta = jnp.einsum(
        "gij,gje->gie", block_diag, grouped, preferred_element_type=jnp.float32
    ) * width ** (-0.5)
    return emb_delta.astype(jnp.bfloat16).reshape(count, feats, width)


def local(
    hash_codes, sample_index, labels, encoder_first, encoder_second, top_weight, score_vector
):
    feat_count = lax.axis_size("feat")
    encoded = (hash_codes[0].astype(jnp.float32) * (2.0 / (BUCKETS - 1)) - 1.0).astype(jnp.bfloat16)
    first_pre = jnp.dot(encoded, encoder_first[0], preferred_element_type=jnp.float32)
    first_hidden = jax.nn.silu(first_pre).astype(jnp.bfloat16)
    row_table = jnp.dot(first_hidden, encoder_second[0], preferred_element_type=jnp.float32).astype(
        jnp.bfloat16
    )
    positions = sample_index[0]
    slot_count = row_table.shape[0]
    emb_width = row_table.shape[1]
    chunk_count = 1
    per_dest = positions.shape[0] // feat_count
    chunk_len = per_dest // chunk_count
    slot_iota = lax.broadcasted_iota(jnp.int32, (1, slot_count), 1)
    label_column = labels[:, 0]
    grad_parts = []
    for chunk in range(chunk_count):
        chunk_positions = positions.reshape(feat_count, per_dest)[
            :, chunk * chunk_len : (chunk + 1) * chunk_len
        ].reshape(-1)
        select = (chunk_positions[:, None] == slot_iota).astype(jnp.bfloat16)
        chosen_rows = (
            jnp.dot(select, row_table, preferred_element_type=jnp.float32)
            .astype(jnp.bfloat16)
            .reshape(feat_count, chunk_len, emb_width)
        )
        picked = lax.all_to_all(
            chosen_rows[:, :, None], "feat", split_axis=0, concat_axis=2, tiled=True
        )[0]
        emb_delta = top_tower(
            picked,
            label_column[chunk * chunk_len : (chunk + 1) * chunk_len],
            top_weight,
            score_vector,
        )
        returned = lax.all_to_all(
            emb_delta[None], "feat", split_axis=2, concat_axis=0, tiled=True
        )
        grad_parts.append(
            jnp.einsum(
                "nu,ne->ue",
                select,
                returned.reshape(-1, emb_width),
                preferred_element_type=jnp.float32,
            )
        )
    row_grads = grad_parts[0]
    for part in grad_parts[1:]:
        row_grads = row_grads + part
    row_delta = row_grads.astype(jnp.bfloat16)
    second_local = jnp.einsum(
        "rk,re->ke", first_hidden, row_delta, preferred_element_type=jnp.float32
    )
    first_back = jnp.einsum(
        "re,ke->rk", row_delta, encoder_second[0], preferred_element_type=jnp.float32
    )
    first_delta = (first_back * silu_slope(first_pre)).astype(jnp.bfloat16)
    group_count = lax.axis_size("samp")
    shard_id = lax.axis_index("samp")
    hid_width = first_delta.shape[1]
    half_width = hid_width // 2
    first_rows = encoded.shape[1] // group_count
    second_rows = second_local.shape[0] // group_count
    second_split = second_local.astype(jnp.bfloat16).astype(jnp.float32).reshape(
        group_count, 2, second_rows // 2, emb_width
    )
    pieces = []
    for side in range(2):
        first_half = jnp.einsum(
            "rh,rk->hk",
            encoded,
            first_delta[:, side * half_width : (side + 1) * half_width],
            preferred_element_type=jnp.float32,
        )
        first_half = first_half.astype(jnp.bfloat16).astype(jnp.float32)
        pieces.append(
            jnp.concatenate(
                [first_half.reshape(group_count, first_rows, half_width), second_split[:, side]],
                axis=2,
            )
        )
    chains = []
    for side, step in ((0, 1), (1, -1)):
        piece_rows = pieces[side].shape[1] // 2
        for part in range(2):
            piece = pieces[side][:, part * piece_rows : (part + 1) * piece_rows]
            acc = lax.dynamic_index_in_dim(
                piece, (shard_id - step) % group_count, 0, keepdims=False
            )
            chains.append([piece, step, acc])
    for hop in range(group_count - 1):
        for chain in chains:
            piece, step, acc = chain
            ring = [(j, (j + step) % group_count) for j in range(group_count)]
            recv = lax.ppermute(acc.astype(jnp.bfloat16), "samp", ring)
            block = (shard_id - step * (hop + 2)) % group_count
            chain[2] = recv.astype(jnp.float32) + lax.dynamic_index_in_dim(
                piece, block, 0, keepdims=False
            )
    results = [
        jnp.concatenate([chains[0][2], chains[1][2]], axis=0),
        jnp.concatenate([chains[2][2], chains[3][2]], axis=0),
    ]
    share_first = jnp.concatenate([part[:, :half_width] for part in results], axis=1)
    share_second = jnp.concatenate([part[:, half_width:] for part in results], axis=0)
    return (row_grads[None], share_first[None], share_second[None])


def solution(mesh):
    return jax.shard_map(
        local,
        mesh=mesh,
        in_specs=(
            P("feat", "samp", None),
            P("feat", "samp"),
            P("feat", "samp"),
            P("feat", None, None),
            P("feat", None, None),
            P(),
            P(),
        ),
        out_specs=(P("feat", "samp", None), P("feat", "samp", None), P("feat", "samp", None)),
        check_vma=False,
    )
```

```python
import jax
import jax.numpy as jnp
from jax import lax
from jax.sharding import PartitionSpec as P

BUCKETS = 4096


loss_scale = 256.0


def silu_slope(inputs):
    logistic = jax.nn.sigmoid(inputs)
    return logistic * (1.0 + inputs * (1.0 - logistic))


def top_tower(picked, label_block, top_weight, score_vector):
    feats, count, width = picked.shape
    pair_dots = (
        jnp.einsum("fne,hne->nfh", picked, picked, preferred_element_type=jnp.float32)
        * width ** (-0.5)
    ).astype(jnp.bfloat16)
    pair_flat = pair_dots.reshape(count, feats * feats)
    top_pre = jnp.dot(pair_flat, top_weight, preferred_element_type=jnp.float32)
    top_hidden = jax.nn.silu(top_pre).astype(jnp.bfloat16)
    logits = jnp.dot(top_hidden, score_vector, preferred_element_type=jnp.float32)
    dlogit = loss_scale * (jax.nn.sigmoid(logits) - label_block.astype(jnp.float32))
    top_delta = (
        dlogit[:, None] * score_vector.astype(jnp.float32)[None, :] * silu_slope(top_pre)
    ).astype(jnp.bfloat16)
    pair_delta = jnp.einsum(
        "nk,jk->nj", top_delta, top_weight, preferred_element_type=jnp.float32
    ).reshape(count, feats, feats)
    pair_sym = (pair_delta + jnp.swapaxes(pair_delta, 1, 2)).astype(jnp.bfloat16)
    emb_delta = jnp.einsum(
        "nfh,hne->fne", pair_sym, picked, preferred_element_type=jnp.float32
    ) * width ** (-0.5)
    return emb_delta.astype(jnp.bfloat16)


def local(
    hash_codes, sample_index, labels, encoder_first, encoder_second, top_weight, score_vector
):
    feat_count = lax.axis_size("feat")
    encoded = (hash_codes[0].astype(jnp.float32) * (2.0 / (BUCKETS - 1)) - 1.0).astype(jnp.bfloat16)
    encoded = lax.optimization_barrier(encoded)
    first_pre = jnp.dot(encoded, encoder_first[0], preferred_element_type=jnp.float32)
    first_hidden = jax.nn.silu(first_pre).astype(jnp.bfloat16)
    row_table = jnp.dot(first_hidden, encoder_second[0], preferred_element_type=jnp.float32).astype(
        jnp.bfloat16
    )
    positions = sample_index[0]
    slot_count = row_table.shape[0]
    emb_width = row_table.shape[1]
    chunk_count = 2
    per_dest = positions.shape[0] // feat_count
    chunk_len = per_dest // chunk_count
    slot_iota = lax.broadcasted_iota(jnp.int32, (1, slot_count), 1)
    label_column = labels[:, 0]
    grad_parts = []
    for chunk in range(chunk_count):
        chunk_positions = positions.reshape(feat_count, per_dest)[
            :, chunk * chunk_len : (chunk + 1) * chunk_len
        ].reshape(-1)
        select = (chunk_positions[:, None] == slot_iota).astype(jnp.bfloat16)
        chosen_rows = (
            jnp.dot(select, row_table, preferred_element_type=jnp.float32)
            .astype(jnp.bfloat16)
            .reshape(feat_count, chunk_len, emb_width)
        )
        picked = lax.all_to_all(chosen_rows, "feat", split_axis=0, concat_axis=0, tiled=True)
        emb_delta = top_tower(
            picked,
            label_column[chunk * chunk_len : (chunk + 1) * chunk_len],
            top_weight,
            score_vector,
        )
        returned = lax.all_to_all(emb_delta, "feat", split_axis=0, concat_axis=0, tiled=True)
        grad_parts.append(
            jnp.einsum(
                "nu,ne->ue",
                select,
                returned.reshape(-1, emb_width),
                preferred_element_type=jnp.float32,
            )
        )
    row_grads = grad_parts[0]
    for part in grad_parts[1:]:
        row_grads = row_grads + part
    row_delta = row_grads.astype(jnp.bfloat16)
    second_local = jnp.einsum(
        "rk,re->ke", first_hidden, row_delta, preferred_element_type=jnp.float32
    )
    first_back = jnp.einsum(
        "re,ke->rk", row_delta, encoder_second[0], preferred_element_type=jnp.float32
    )
    first_delta = (first_back * silu_slope(first_pre)).astype(jnp.bfloat16)
    group_count = lax.axis_size("samp")
    shard_id = lax.axis_index("samp")
    hid_width = first_delta.shape[1]
    half_width = hid_width // 2
    first_rows = encoded.shape[1] // group_count
    second_rows = second_local.shape[0] // group_count
    second_split = second_local.astype(jnp.bfloat16).astype(jnp.float32).reshape(
        group_count, 2, second_rows // 2, emb_width
    )
    pieces = []
    for side in range(2):
        first_half = jnp.einsum(
            "rh,rk->hk",
            encoded,
            first_delta[:, side * half_width : (side + 1) * half_width],
            preferred_element_type=jnp.float32,
        )
        first_half = first_half.astype(jnp.bfloat16).astype(jnp.float32)
        pieces.append(
            jnp.concatenate(
                [first_half.reshape(group_count, first_rows, half_width), second_split[:, side]],
                axis=2,
            )
        )
    chains = []
    for side, step in ((0, 1), (1, -1)):
        piece_rows = pieces[side].shape[1] // 2
        for part in range(2):
            piece = pieces[side][:, part * piece_rows : (part + 1) * piece_rows]
            acc = lax.dynamic_index_in_dim(
                piece, (shard_id - step) % group_count, 0, keepdims=False
            )
            chains.append([piece, step, acc])
    for hop in range(group_count - 1):
        for chain in chains:
            piece, step, acc = chain
            ring = [(j, (j + step) % group_count) for j in range(group_count)]
            recv = lax.ppermute(acc.astype(jnp.bfloat16), "samp", ring)
            block = (shard_id - step * (hop + 2)) % group_count
            chain[2] = recv.astype(jnp.float32) + lax.dynamic_index_in_dim(
                piece, block, 0, keepdims=False
            )
    results = [
        jnp.concatenate([chains[0][2], chains[1][2]], axis=0),
        jnp.concatenate([chains[2][2], chains[3][2]], axis=0),
    ]
    share_first = jnp.concatenate([part[:, :half_width] for part in results], axis=1)
    share_second = jnp.concatenate([part[:, half_width:] for part in results], axis=0)
    return (row_grads[None], share_first[None], share_second[None])


def solution(mesh):
    return jax.shard_map(
        local,
        mesh=mesh,
        in_specs=(
            P("feat", "samp", None),
            P("feat", "samp"),
            P("feat", "samp"),
            P("feat", None, None),
            P("feat", None, None),
            P(),
            P(),
        ),
        out_specs=(P("feat", "samp", None), P("feat", "samp", None), P("feat", "samp", None)),
        check_vma=False,
    )
```

```python
import jax
import jax.numpy as jnp
from jax import lax
from jax.sharding import PartitionSpec as P

BUCKETS = 4096


loss_scale = 256.0


def silu_slope(inputs):
    logistic = jax.nn.sigmoid(inputs)
    return logistic * (1.0 + inputs * (1.0 - logistic))


def top_tower(picked, label_block, top_weight, score_vector):
    feats, count, width = picked.shape
    pair_dots = (
        jnp.einsum("fne,hne->nfh", picked, picked, preferred_element_type=jnp.float32)
        * width ** (-0.5)
    ).astype(jnp.bfloat16)
    pair_flat = pair_dots.reshape(count, feats * feats)
    top_pre = jnp.dot(pair_flat, top_weight, preferred_element_type=jnp.float32)
    top_hidden = jax.nn.silu(top_pre).astype(jnp.bfloat16)
    logits = jnp.dot(top_hidden, score_vector, preferred_element_type=jnp.float32)
    dlogit = loss_scale * (jax.nn.sigmoid(logits) - label_block.astype(jnp.float32))
    top_delta = (
        dlogit[:, None] * score_vector.astype(jnp.float32)[None, :] * silu_slope(top_pre)
    ).astype(jnp.bfloat16)
    pair_delta = jnp.einsum(
        "nk,jk->nj", top_delta, top_weight, preferred_element_type=jnp.float32
    ).reshape(count, feats, feats)
    pair_sym = (pair_delta + jnp.swapaxes(pair_delta, 1, 2)).astype(jnp.bfloat16)
    emb_delta = jnp.einsum(
        "nfh,hne->fne", pair_sym, picked, preferred_element_type=jnp.float32
    ) * width ** (-0.5)
    return emb_delta.astype(jnp.bfloat16)


def local(
    hash_codes, sample_index, labels, encoder_first, encoder_second, top_weight, score_vector
):
    feat_count = lax.axis_size("feat")
    encoded = (hash_codes[0].astype(jnp.float32) * (2.0 / (BUCKETS - 1)) - 1.0).astype(jnp.bfloat16)
    first_pre = jnp.dot(encoded, encoder_first[0], preferred_element_type=jnp.float32)
    first_hidden = jax.nn.silu(first_pre).astype(jnp.bfloat16)
    row_table = jnp.dot(first_hidden, encoder_second[0], preferred_element_type=jnp.float32).astype(
        jnp.bfloat16
    )
    positions = sample_index[0]
    slot_count = row_table.shape[0]
    emb_width = row_table.shape[1]
    chunk_count = 2
    per_dest = positions.shape[0] // feat_count
    chunk_len = per_dest // chunk_count
    slot_iota = lax.broadcasted_iota(jnp.int32, (1, slot_count), 1)
    label_column = labels[:, 0]
    grad_parts = []
    for chunk in range(chunk_count):
        chunk_positions = positions.reshape(feat_count, per_dest)[
            :, chunk * chunk_len : (chunk + 1) * chunk_len
        ].reshape(-1)
        select = (chunk_positions[:, None] == slot_iota).astype(jnp.bfloat16)
        chosen_rows = (
            jnp.dot(select, row_table, preferred_element_type=jnp.float32)
            .astype(jnp.bfloat16)
            .reshape(feat_count, chunk_len, emb_width)
        )
        picked = lax.all_to_all(chosen_rows, "feat", split_axis=0, concat_axis=0, tiled=True)
        emb_delta = top_tower(
            picked,
            label_column[chunk * chunk_len : (chunk + 1) * chunk_len],
            top_weight,
            score_vector,
        )
        returned = lax.all_to_all(emb_delta, "feat", split_axis=0, concat_axis=0, tiled=True)
        grad_parts.append(
            jnp.einsum(
                "nu,ne->ue",
                select,
                returned.reshape(-1, emb_width),
                preferred_element_type=jnp.float32,
            )
        )
    row_grads = grad_parts[0]
    for part in grad_parts[1:]:
        row_grads = row_grads + part
    row_delta = row_grads.astype(jnp.bfloat16)
    second_local = jnp.einsum(
        "rk,re->ke", first_hidden, row_delta, preferred_element_type=jnp.float32
    )
    first_back = jnp.einsum(
        "re,ke->rk", row_delta, encoder_second[0], preferred_element_type=jnp.float32
    )
    first_delta = (first_back * silu_slope(first_pre)).astype(jnp.bfloat16)
    group_count = lax.axis_size("samp")
    shard_id = lax.axis_index("samp")
    hid_width = first_delta.shape[1]
    half_width = hid_width // 2
    first_rows = encoded.shape[1] // group_count
    second_rows = second_local.shape[0] // group_count
    second_split = second_local.astype(jnp.bfloat16).astype(jnp.float32).reshape(
        group_count, 2, second_rows // 2, emb_width
    )
    def start_chain(piece, step):
        acc = lax.dynamic_index_in_dim(piece, (shard_id - step) % group_count, 0, keepdims=False)
        return [piece, step, acc]

    second_chains = [
        start_chain(second_split[:, side], step) for side, step in ((0, 1), (1, -1))
    ]
    first_chains = []
    for side, step in ((0, 1), (1, -1)):
        first_half = jnp.einsum(
            "rh,rk->hk",
            encoded,
            first_delta[:, side * half_width : (side + 1) * half_width],
            preferred_element_type=jnp.float32,
        )
        first_half = first_half.astype(jnp.bfloat16).astype(jnp.float32)
        first_half = first_half.reshape(group_count, first_rows, half_width)
        piece_rows = first_rows // 2
        for part in range(2):
            first_chains.append(
                start_chain(first_half[:, part * piece_rows : (part + 1) * piece_rows], step)
            )
    chains = second_chains + first_chains
    for hop in range(group_count - 1):
        for chain in chains:
            piece, step, acc = chain
            ring = [(j, (j + step) % group_count) for j in range(group_count)]
            recv = lax.ppermute(acc.astype(jnp.bfloat16), "samp", ring)
            block = (shard_id - step * (hop + 2)) % group_count
            chain[2] = recv.astype(jnp.float32) + lax.dynamic_index_in_dim(
                piece, block, 0, keepdims=False
            )
    share_second = jnp.concatenate([chain[2] for chain in second_chains], axis=0)
    share_first = jnp.concatenate(
        [
            jnp.concatenate([first_chains[0][2], first_chains[1][2]], axis=0),
            jnp.concatenate([first_chains[2][2], first_chains[3][2]], axis=0),
        ],
        axis=1,
    )
    return (row_grads[None], share_first[None], share_second[None])


def solution(mesh):
    return jax.shard_map(
        local,
        mesh=mesh,
        in_specs=(
            P("feat", "samp", None),
            P("feat", "samp"),
            P("feat", "samp"),
            P("feat", None, None),
            P("feat", None, None),
            P(),
            P(),
        ),
        out_specs=(P("feat", "samp", None), P("feat", "samp", None), P("feat", "samp", None)),
        check_vma=False,
    )
```

```python
import jax
import jax.numpy as jnp
from jax import lax
from jax.sharding import PartitionSpec as P

BUCKETS = 4096


loss_scale = 256.0


def silu_slope(inputs):
    logistic = jax.nn.sigmoid(inputs)
    return logistic * (1.0 + inputs * (1.0 - logistic))


def top_tower(picked, label_block, top_weight, score_vector):
    feats, count, width = picked.shape
    pair_dots = (
        jnp.einsum("fne,hne->nfh", picked, picked, preferred_element_type=jnp.float32)
        * width ** (-0.5)
    ).astype(jnp.bfloat16)
    pair_flat = pair_dots.reshape(count, feats * feats)
    top_pre = jnp.dot(pair_flat, top_weight, preferred_element_type=jnp.float32)
    top_hidden = jax.nn.silu(top_pre).astype(jnp.bfloat16)
    logits = jnp.dot(top_hidden, score_vector, preferred_element_type=jnp.float32)
    dlogit = loss_scale * (jax.nn.sigmoid(logits) - label_block.astype(jnp.float32))
    top_delta = (
        dlogit[:, None] * score_vector.astype(jnp.float32)[None, :] * silu_slope(top_pre)
    ).astype(jnp.bfloat16)
    pair_delta = jnp.einsum(
        "nk,jk->nj", top_delta, top_weight, preferred_element_type=jnp.float32
    ).reshape(count, feats, feats)
    pair_sym = (pair_delta + jnp.swapaxes(pair_delta, 1, 2)).astype(jnp.bfloat16)
    emb_delta = jnp.einsum(
        "nfh,hne->fne", pair_sym, picked, preferred_element_type=jnp.float32
    ) * width ** (-0.5)
    return emb_delta.astype(jnp.bfloat16)


def local(
    hash_codes, sample_index, labels, encoder_first, encoder_second, top_weight, score_vector
):
    feat_count = lax.axis_size("feat")
    encoded = (hash_codes[0].astype(jnp.float32) * (2.0 / (BUCKETS - 1)) - 1.0).astype(jnp.bfloat16)
    first_pre = jnp.dot(encoded, encoder_first[0], preferred_element_type=jnp.float32)
    first_hidden = jax.nn.silu(first_pre).astype(jnp.bfloat16)
    row_table = jnp.dot(first_hidden, encoder_second[0], preferred_element_type=jnp.float32).astype(
        jnp.bfloat16
    )
    positions = sample_index[0]
    slot_count = row_table.shape[0]
    emb_width = row_table.shape[1]
    chunk_count = 2
    per_dest = positions.shape[0] // feat_count
    chunk_len = per_dest // chunk_count
    slot_iota = lax.broadcasted_iota(jnp.int32, (1, slot_count), 1)
    label_column = labels[:, 0]
    grad_parts = []
    for chunk in range(chunk_count):
        chunk_positions = positions.reshape(feat_count, per_dest)[
            :, chunk * chunk_len : (chunk + 1) * chunk_len
        ].reshape(-1)
        select = (chunk_positions[:, None] == slot_iota).astype(jnp.bfloat16)
        chosen_rows = (
            jnp.dot(select, row_table, preferred_element_type=jnp.float32)
            .astype(jnp.bfloat16)
            .reshape(feat_count, chunk_len, emb_width)
        )
        picked = lax.all_to_all(chosen_rows, "feat", split_axis=0, concat_axis=0, tiled=True)
        emb_delta = top_tower(
            picked,
            label_column[chunk * chunk_len : (chunk + 1) * chunk_len],
            top_weight,
            score_vector,
        )
        returned = lax.all_to_all(emb_delta, "feat", split_axis=0, concat_axis=0, tiled=True)
        grad_parts.append(
            jnp.einsum(
                "nu,ne->ue",
                select,
                returned.reshape(-1, emb_width),
                preferred_element_type=jnp.float32,
            )
        )
    row_grads = grad_parts[0]
    for part in grad_parts[1:]:
        row_grads = row_grads + part
    row_delta = row_grads.astype(jnp.bfloat16)
    second_local = jnp.einsum(
        "rk,re->ke", first_hidden, row_delta, preferred_element_type=jnp.float32
    )
    first_back = jnp.einsum(
        "re,ke->rk", row_delta, encoder_second[0], preferred_element_type=jnp.float32
    )
    first_delta = (first_back * silu_slope(first_pre)).astype(jnp.bfloat16)
    group_count = lax.axis_size("samp")
    shard_id = lax.axis_index("samp")
    hid_width = first_delta.shape[1]
    half_width = hid_width // 2
    first_rows = encoded.shape[1] // group_count
    second_rows = second_local.shape[0] // group_count
    second_split = second_local.astype(jnp.bfloat16).astype(jnp.float32).reshape(
        group_count, 2, second_rows // 2, emb_width
    )
    pieces = []
    for side in range(2):
        first_half = jnp.einsum(
            "rh,rk->hk",
            encoded,
            first_delta[:, side * half_width : (side + 1) * half_width],
            preferred_element_type=jnp.float32,
        )
        first_half = first_half.astype(jnp.bfloat16).astype(jnp.float32)
        pieces.append(
            jnp.concatenate(
                [first_half.reshape(group_count, first_rows, half_width), second_split[:, side]],
                axis=2,
            )
        )
    chains = []
    for side, step in ((0, 1), (1, -1)):
        piece_rows = pieces[side].shape[1] // 4
        for part in range(4):
            piece = pieces[side][:, part * piece_rows : (part + 1) * piece_rows]
            acc = lax.dynamic_index_in_dim(
                piece, (shard_id - step) % group_count, 0, keepdims=False
            )
            chains.append([piece, step, acc])
    for hop in range(group_count - 1):
        for chain in chains:
            piece, step, acc = chain
            ring = [(j, (j + step) % group_count) for j in range(group_count)]
            recv = lax.ppermute(acc.astype(jnp.bfloat16), "samp", ring)
            block = (shard_id - step * (hop + 2)) % group_count
            chain[2] = recv.astype(jnp.float32) + lax.dynamic_index_in_dim(
                piece, block, 0, keepdims=False
            )
    results = [
        jnp.concatenate([chain[2] for chain in chains[:4]], axis=0),
        jnp.concatenate([chain[2] for chain in chains[4:]], axis=0),
    ]
    share_first = jnp.concatenate([part[:, :half_width] for part in results], axis=1)
    share_second = jnp.concatenate([part[:, half_width:] for part in results], axis=0)
    return (row_grads[None], share_first[None], share_second[None])


def solution(mesh):
    return jax.shard_map(
        local,
        mesh=mesh,
        in_specs=(
            P("feat", "samp", None),
            P("feat", "samp"),
            P("feat", "samp"),
            P("feat", None, None),
            P("feat", None, None),
            P(),
            P(),
        ),
        out_specs=(P("feat", "samp", None), P("feat", "samp", None), P("feat", "samp", None)),
        check_vma=False,
    )
```

```python
import jax
import jax.numpy as jnp
from jax import lax
from jax.sharding import PartitionSpec as P

BUCKETS = 4096


loss_scale = 256.0


def silu_slope(inputs):
    logistic = jax.nn.sigmoid(inputs)
    return logistic * (1.0 + inputs * (1.0 - logistic))


def top_tower(picked, label_block, top_weight, score_vector):
    feats, count, width = picked.shape
    pair_dots = (
        jnp.einsum("fne,hne->nfh", picked, picked, preferred_element_type=jnp.float32)
        * width ** (-0.5)
    ).astype(jnp.bfloat16)
    pair_flat = pair_dots.reshape(count, feats * feats)
    top_pre = jnp.dot(pair_flat, top_weight, preferred_element_type=jnp.float32)
    top_hidden = jax.nn.silu(top_pre).astype(jnp.bfloat16)
    logits = jnp.dot(top_hidden, score_vector, preferred_element_type=jnp.float32)
    dlogit = loss_scale * (jax.nn.sigmoid(logits) - label_block.astype(jnp.float32))
    top_delta = (
        dlogit[:, None] * score_vector.astype(jnp.float32)[None, :] * silu_slope(top_pre)
    ).astype(jnp.bfloat16)
    pair_delta = jnp.einsum(
        "nk,jk->nj", top_delta, top_weight, preferred_element_type=jnp.float32
    ).reshape(count, feats, feats)
    pair_sym = (pair_delta + jnp.swapaxes(pair_delta, 1, 2)).astype(jnp.bfloat16)
    emb_delta = jnp.einsum(
        "nfh,hne->fne", pair_sym, picked, preferred_element_type=jnp.float32
    ) * width ** (-0.5)
    return emb_delta.astype(jnp.bfloat16)


def local(
    hash_codes, sample_index, labels, encoder_first, encoder_second, top_weight, score_vector
):
    feat_count = lax.axis_size("feat")
    encoded = (hash_codes[0].astype(jnp.float32) * (2.0 / (BUCKETS - 1)) - 1.0).astype(jnp.bfloat16)
    first_pre = jnp.dot(encoded, encoder_first[0], preferred_element_type=jnp.float32)
    first_hidden = jax.nn.silu(first_pre).astype(jnp.bfloat16)
    row_table = jnp.dot(first_hidden, encoder_second[0], preferred_element_type=jnp.float32).astype(
        jnp.bfloat16
    )
    first_slope = lax.optimization_barrier(silu_slope(first_pre))
    positions = sample_index[0]
    slot_count = row_table.shape[0]
    emb_width = row_table.shape[1]
    chunk_count = 2
    per_dest = positions.shape[0] // feat_count
    chunk_len = per_dest // chunk_count
    slot_iota = lax.broadcasted_iota(jnp.int32, (1, slot_count), 1)
    label_column = labels[:, 0]
    grad_parts = []
    for chunk in range(chunk_count):
        chunk_positions = positions.reshape(feat_count, per_dest)[
            :, chunk * chunk_len : (chunk + 1) * chunk_len
        ].reshape(-1)
        select = (chunk_positions[:, None] == slot_iota).astype(jnp.bfloat16)
        chosen_rows = (
            jnp.dot(select, row_table, preferred_element_type=jnp.float32)
            .astype(jnp.bfloat16)
            .reshape(feat_count, chunk_len, emb_width)
        )
        picked = lax.all_to_all(chosen_rows, "feat", split_axis=0, concat_axis=0, tiled=True)
        emb_delta = top_tower(
            picked,
            label_column[chunk * chunk_len : (chunk + 1) * chunk_len],
            top_weight,
            score_vector,
        )
        returned = lax.all_to_all(emb_delta, "feat", split_axis=0, concat_axis=0, tiled=True)
        grad_parts.append(
            jnp.einsum(
                "nu,ne->ue",
                select,
                returned.reshape(-1, emb_width),
                preferred_element_type=jnp.float32,
            )
        )
    row_grads = grad_parts[0]
    for part in grad_parts[1:]:
        row_grads = row_grads + part
    row_delta = row_grads.astype(jnp.bfloat16)
    second_local = jnp.einsum(
        "rk,re->ke", first_hidden, row_delta, preferred_element_type=jnp.float32
    )
    first_back = jnp.einsum(
        "re,ke->rk", row_delta, encoder_second[0], preferred_element_type=jnp.float32
    )
    first_delta = (first_back * first_slope).astype(jnp.bfloat16)
    group_count = lax.axis_size("samp")
    shard_id = lax.axis_index("samp")
    hid_width = first_delta.shape[1]
    half_width = hid_width // 2
    first_rows = encoded.shape[1] // group_count
    second_rows = second_local.shape[0] // group_count
    second_split = second_local.astype(jnp.bfloat16).astype(jnp.float32).reshape(
        group_count, 2, second_rows // 2, emb_width
    )
    pieces = []
    for side in range(2):
        first_half = jnp.einsum(
            "rh,rk->hk",
            encoded,
            first_delta[:, side * half_width : (side + 1) * half_width],
            preferred_element_type=jnp.float32,
        )
        first_half = first_half.astype(jnp.bfloat16).astype(jnp.float32)
        pieces.append(
            jnp.concatenate(
                [first_half.reshape(group_count, first_rows, half_width), second_split[:, side]],
                axis=2,
            )
        )
    chains = []
    for side, step in ((0, 1), (1, -1)):
        piece_rows = pieces[side].shape[1] // 2
        for part in range(2):
            piece = pieces[side][:, part * piece_rows : (part + 1) * piece_rows]
            acc = lax.dynamic_index_in_dim(
                piece, (shard_id - step) % group_count, 0, keepdims=False
            )
            chains.append([piece, step, acc])
    for hop in range(group_count - 1):
        for chain in chains:
            piece, step, acc = chain
            ring = [(j, (j + step) % group_count) for j in range(group_count)]
            recv = lax.ppermute(acc.astype(jnp.bfloat16), "samp", ring)
            block = (shard_id - step * (hop + 2)) % group_count
            chain[2] = recv.astype(jnp.float32) + lax.dynamic_index_in_dim(
                piece, block, 0, keepdims=False
            )
    results = [
        jnp.concatenate([chains[0][2], chains[1][2]], axis=0),
        jnp.concatenate([chains[2][2], chains[3][2]], axis=0),
    ]
    share_first = jnp.concatenate([part[:, :half_width] for part in results], axis=1)
    share_second = jnp.concatenate([part[:, half_width:] for part in results], axis=0)
    return (row_grads[None], share_first[None], share_second[None])


def solution(mesh):
    return jax.shard_map(
        local,
        mesh=mesh,
        in_specs=(
            P("feat", "samp", None),
            P("feat", "samp"),
            P("feat", "samp"),
            P("feat", None, None),
            P("feat", None, None),
            P(),
            P(),
        ),
        out_specs=(P("feat", "samp", None), P("feat", "samp", None), P("feat", "samp", None)),
        check_vma=False,
    )
```

```python
import jax
import jax.numpy as jnp
from jax import lax
from jax.sharding import PartitionSpec as P

BUCKETS = 4096


loss_scale = 256.0


def silu_slope(inputs):
    logistic = jax.nn.sigmoid(inputs)
    return logistic * (1.0 + inputs * (1.0 - logistic))


def top_tower(picked, label_block, top_weight, score_vector):
    feats, count, width = picked.shape
    pair_dots = (
        jnp.einsum("fne,hne->nfh", picked, picked, preferred_element_type=jnp.float32)
        * width ** (-0.5)
    ).astype(jnp.bfloat16)
    pair_flat = pair_dots.reshape(count, feats * feats)
    top_pre = jnp.dot(pair_flat, top_weight, preferred_element_type=jnp.float32)
    top_hidden = jax.nn.silu(top_pre).astype(jnp.bfloat16)
    logits = jnp.dot(top_hidden, score_vector, preferred_element_type=jnp.float32)
    dlogit = loss_scale * (jax.nn.sigmoid(logits) - label_block.astype(jnp.float32))
    top_delta = (
        dlogit[:, None] * score_vector.astype(jnp.float32)[None, :] * silu_slope(top_pre)
    ).astype(jnp.bfloat16)
    pair_delta = jnp.einsum(
        "nk,jk->nj", top_delta, top_weight, preferred_element_type=jnp.float32
    ).reshape(count, feats, feats)
    pair_sym = (pair_delta + jnp.swapaxes(pair_delta, 1, 2)).astype(jnp.bfloat16)
    emb_delta = jnp.einsum(
        "nfh,hne->fne", pair_sym, picked, preferred_element_type=jnp.float32
    ) * width ** (-0.5)
    return emb_delta.astype(jnp.bfloat16)


def local(
    hash_codes, sample_index, labels, encoder_first, encoder_second, top_weight, score_vector
):
    feat_count = lax.axis_size("feat")
    encoded = (hash_codes[0].astype(jnp.float32) * (2.0 / (BUCKETS - 1)) - 1.0).astype(jnp.bfloat16)
    first_pre = jnp.dot(encoded, encoder_first[0], preferred_element_type=jnp.float32)
    first_hidden = jax.nn.silu(first_pre).astype(jnp.bfloat16)
    row_table = jnp.dot(first_hidden, encoder_second[0], preferred_element_type=jnp.float32).astype(
        jnp.bfloat16
    )
    positions = sample_index[0]
    slot_count = row_table.shape[0]
    emb_width = row_table.shape[1]
    chunk_count = 2
    per_dest = positions.shape[0] // feat_count
    chunk_len = per_dest // chunk_count
    slot_column = lax.broadcasted_iota(jnp.int32, (slot_count, 1), 0)
    index_rows = sample_index.reshape(1, feat_count, per_dest)
    label_column = labels[:, 0]
    grad_parts = []
    for chunk in range(chunk_count):
        chunk_positions = index_rows[:, :, chunk * chunk_len : (chunk + 1) * chunk_len].reshape(
            1, feat_count * chunk_len
        )
        select = (slot_column == chunk_positions).astype(jnp.bfloat16)
        chosen_rows = (
            jnp.einsum("un,ue->ne", select, row_table, preferred_element_type=jnp.float32)
            .astype(jnp.bfloat16)
            .reshape(feat_count, chunk_len, emb_width)
        )
        picked = lax.all_to_all(chosen_rows, "feat", split_axis=0, concat_axis=0, tiled=True)
        emb_delta = top_tower(
            picked,
            label_column[chunk * chunk_len : (chunk + 1) * chunk_len],
            top_weight,
            score_vector,
        )
        returned = lax.all_to_all(emb_delta, "feat", split_axis=0, concat_axis=0, tiled=True)
        grad_parts.append(
            jnp.dot(select, returned.reshape(-1, emb_width), preferred_element_type=jnp.float32)
        )
    row_grads = grad_parts[0]
    for part in grad_parts[1:]:
        row_grads = row_grads + part
    row_delta = row_grads.astype(jnp.bfloat16)
    second_local = jnp.einsum(
        "rk,re->ke", first_hidden, row_delta, preferred_element_type=jnp.float32
    )
    first_back = jnp.einsum(
        "re,ke->rk", row_delta, encoder_second[0], preferred_element_type=jnp.float32
    )
    first_delta = (first_back * silu_slope(first_pre)).astype(jnp.bfloat16)
    group_count = lax.axis_size("samp")
    shard_id = lax.axis_index("samp")
    hid_width = first_delta.shape[1]
    half_width = hid_width // 2
    first_rows = encoded.shape[1] // group_count
    second_rows = second_local.shape[0] // group_count
    second_split = second_local.astype(jnp.bfloat16).astype(jnp.float32).reshape(
        group_count, 2, second_rows // 2, emb_width
    )
    pieces = []
    for side in range(2):
        first_half = jnp.einsum(
            "rh,rk->hk",
            encoded,
            first_delta[:, side * half_width : (side + 1) * half_width],
            preferred_element_type=jnp.float32,
        )
        first_half = first_half.astype(jnp.bfloat16).astype(jnp.float32)
        pieces.append(
            jnp.concatenate(
                [first_half.reshape(group_count, first_rows, half_width), second_split[:, side]],
                axis=2,
            )
        )
    chains = []
    for side, step in ((0, 1), (1, -1)):
        piece_rows = pieces[side].shape[1] // 2
        for part in range(2):
            piece = pieces[side][:, part * piece_rows : (part + 1) * piece_rows]
            acc = lax.dynamic_index_in_dim(
                piece, (shard_id - step) % group_count, 0, keepdims=False
            )
            chains.append([piece, step, acc])
    for hop in range(group_count - 1):
        for chain in chains:
            piece, step, acc = chain
            ring = [(j, (j + step) % group_count) for j in range(group_count)]
            recv = lax.ppermute(acc.astype(jnp.bfloat16), "samp", ring)
            block = (shard_id - step * (hop + 2)) % group_count
            chain[2] = recv.astype(jnp.float32) + lax.dynamic_index_in_dim(
                piece, block, 0, keepdims=False
            )
    results = [
        jnp.concatenate([chains[0][2], chains[1][2]], axis=0),
        jnp.concatenate([chains[2][2], chains[3][2]], axis=0),
    ]
    share_first = jnp.concatenate([part[:, :half_width] for part in results], axis=1)
    share_second = jnp.concatenate([part[:, half_width:] for part in results], axis=0)
    return (row_grads[None], share_first[None], share_second[None])


def solution(mesh):
    return jax.shard_map(
        local,
        mesh=mesh,
        in_specs=(
            P("feat", "samp", None),
            P("feat", "samp"),
            P("feat", "samp"),
            P("feat", None, None),
            P("feat", None, None),
            P(),
            P(),
        ),
        out_specs=(P("feat", "samp", None), P("feat", "samp", None), P("feat", "samp", None)),
        check_vma=False,
    )
```

```python
import jax
import jax.numpy as jnp
from jax import lax
from jax.sharding import PartitionSpec as P

BUCKETS = 4096


loss_scale = 256.0


def silu_slope(inputs):
    logistic = jax.nn.sigmoid(inputs)
    return logistic * (1.0 + inputs * (1.0 - logistic))


def top_tower(picked, label_block, top_weight, score_vector):
    feats, count, width = picked.shape
    pair_dots = (
        jnp.einsum("fne,hne->nfh", picked, picked, preferred_element_type=jnp.float32)
        * width ** (-0.5)
    ).astype(jnp.bfloat16)
    pair_flat = pair_dots.reshape(count, feats * feats)
    top_pre = jnp.dot(pair_flat, top_weight, preferred_element_type=jnp.float32)
    top_hidden = jax.nn.silu(top_pre).astype(jnp.bfloat16)
    logits = jnp.dot(top_hidden, score_vector, preferred_element_type=jnp.float32)
    dlogit = loss_scale * (jax.nn.sigmoid(logits) - label_block.astype(jnp.float32))
    top_delta = (
        dlogit[:, None] * score_vector.astype(jnp.float32)[None, :] * silu_slope(top_pre)
    ).astype(jnp.bfloat16)
    pair_delta = jnp.einsum(
        "nk,jk->nj", top_delta, top_weight, preferred_element_type=jnp.float32
    ).reshape(count, feats, feats)
    pair_sym = (pair_delta + jnp.swapaxes(pair_delta, 1, 2)).astype(jnp.bfloat16)
    emb_delta = jnp.einsum(
        "nfh,hne->fne", pair_sym, picked, preferred_element_type=jnp.float32
    ) * width ** (-0.5)
    return emb_delta.astype(jnp.bfloat16)


def local(
    hash_codes, sample_index, labels, encoder_first, encoder_second, top_weight, score_vector
):
    feat_count = lax.axis_size("feat")
    encoded = (hash_codes[0].astype(jnp.float32) * (2.0 / (BUCKETS - 1)) - 1.0).astype(jnp.bfloat16)
    first_pre = jnp.dot(encoded, encoder_first[0], preferred_element_type=jnp.float32)
    first_hidden = jax.nn.silu(first_pre).astype(jnp.bfloat16)
    row_table = jnp.dot(first_hidden, encoder_second[0], preferred_element_type=jnp.float32).astype(
        jnp.bfloat16
    )
    positions = sample_index[0]
    slot_count = row_table.shape[0]
    emb_width = row_table.shape[1]
    chunk_count = 2
    per_dest = positions.shape[0] // feat_count
    chunk_len = per_dest // chunk_count
    slot_iota = lax.broadcasted_iota(jnp.int32, (1, slot_count), 1)
    label_column = labels[:, 0]
    grad_parts = []
    for chunk in range(chunk_count):
        chunk_positions = positions.reshape(feat_count, per_dest)[
            :, chunk * chunk_len : (chunk + 1) * chunk_len
        ].reshape(-1)
        select = (chunk_positions[:, None] == slot_iota).astype(jnp.bfloat16)
        chosen_rows = (
            jnp.dot(select, row_table, preferred_element_type=jnp.float32)
            .astype(jnp.bfloat16)
            .reshape(feat_count, chunk_len, emb_width)
        )
        picked = lax.all_to_all(chosen_rows, "feat", split_axis=0, concat_axis=0, tiled=True)
        emb_delta = top_tower(
            picked,
            label_column[chunk * chunk_len : (chunk + 1) * chunk_len],
            top_weight,
            score_vector,
        )
        returned = lax.all_to_all(emb_delta, "feat", split_axis=0, concat_axis=0, tiled=True)
        grad_parts.append(
            jnp.einsum(
                "nu,ne->ue",
                select,
                returned.reshape(-1, emb_width),
                preferred_element_type=jnp.float32,
            )
        )
    row_grads = grad_parts[0]
    for part in grad_parts[1:]:
        row_grads = row_grads + part
    row_delta = row_grads.astype(jnp.bfloat16)
    second_local = jnp.einsum(
        "rk,re->ke", first_hidden, row_delta, preferred_element_type=jnp.float32
    )
    first_back = jnp.einsum(
        "re,ke->rk", row_delta, encoder_second[0], preferred_element_type=jnp.float32
    )
    first_delta = (first_back * silu_slope(first_pre)).astype(jnp.bfloat16)
    group_count = lax.axis_size("samp")
    shard_id = lax.axis_index("samp")
    hid_width = first_delta.shape[1]
    half_width = hid_width // 2
    first_rows = encoded.shape[1] // group_count
    share_second = lax.psum_scatter(
        second_local.astype(jnp.bfloat16), "samp", scatter_dimension=0, tiled=True
    ).astype(jnp.float32)
    pieces = []
    for side in range(2):
        first_half = jnp.einsum(
            "rh,rk->hk",
            encoded,
            first_delta[:, side * half_width : (side + 1) * half_width],
            preferred_element_type=jnp.float32,
        )
        first_half = first_half.astype(jnp.bfloat16).astype(jnp.float32)
        pieces.append(first_half.reshape(group_count, first_rows, half_width))
    chains = []
    for side, step in ((0, 1), (1, -1)):
        piece_rows = pieces[side].shape[1] // 2
        for part in range(2):
            piece = pieces[side][:, part * piece_rows : (part + 1) * piece_rows]
            acc = lax.dynamic_index_in_dim(
                piece, (shard_id - step) % group_count, 0, keepdims=False
            )
            chains.append([piece, step, acc])
    for hop in range(group_count - 1):
        for chain in chains:
            piece, step, acc = chain
            ring = [(j, (j + step) % group_count) for j in range(group_count)]
            recv = lax.ppermute(acc.astype(jnp.bfloat16), "samp", ring)
            block = (shard_id - step * (hop + 2)) % group_count
            chain[2] = recv.astype(jnp.float32) + lax.dynamic_index_in_dim(
                piece, block, 0, keepdims=False
            )
    results = [
        jnp.concatenate([chains[0][2], chains[1][2]], axis=0),
        jnp.concatenate([chains[2][2], chains[3][2]], axis=0),
    ]
    share_first = jnp.concatenate(results, axis=1)
    return (row_grads[None], share_first[None], share_second[None])


def solution(mesh):
    return jax.shard_map(
        local,
        mesh=mesh,
        in_specs=(
            P("feat", "samp", None),
            P("feat", "samp"),
            P("feat", "samp"),
            P("feat", None, None),
            P("feat", None, None),
            P(),
            P(),
        ),
        out_specs=(P("feat", "samp", None), P("feat", "samp", None), P("feat", "samp", None)),
        check_vma=False,
    )
```

```python
import jax
import jax.numpy as jnp
from jax import lax
from jax.sharding import PartitionSpec as P

BUCKETS = 4096


loss_scale = 256.0


def silu_slope(inputs):
    logistic = jax.nn.sigmoid(inputs)
    return logistic * (1.0 + inputs * (1.0 - logistic))


def top_tower(picked, label_block, top_weight, score_vector):
    feats, count, width = picked.shape
    pair_dots = (
        jnp.einsum("fne,hne->nfh", picked, picked, preferred_element_type=jnp.float32)
        * width ** (-0.5)
    ).astype(jnp.bfloat16)
    pair_flat = pair_dots.reshape(count, feats * feats)
    top_pre = jnp.dot(pair_flat, top_weight, preferred_element_type=jnp.float32)
    top_hidden = jax.nn.silu(top_pre).astype(jnp.bfloat16)
    logits = jnp.dot(top_hidden, score_vector, preferred_element_type=jnp.float32)
    dlogit = loss_scale * (jax.nn.sigmoid(logits) - label_block.astype(jnp.float32))
    top_delta = (
        dlogit[:, None] * score_vector.astype(jnp.float32)[None, :] * silu_slope(top_pre)
    ).astype(jnp.bfloat16)
    pair_delta = jnp.einsum(
        "nk,jk->nj", top_delta, top_weight, preferred_element_type=jnp.float32
    ).reshape(count, feats, feats)
    pair_sym = (pair_delta + jnp.swapaxes(pair_delta, 1, 2)).astype(jnp.bfloat16)
    emb_delta = jnp.einsum(
        "nfh,hne->fne", pair_sym, picked, preferred_element_type=jnp.float32
    ) * width ** (-0.5)
    return emb_delta.astype(jnp.bfloat16)


def local(
    hash_codes, sample_index, labels, encoder_first, encoder_second, top_weight, score_vector
):
    feat_count = lax.axis_size("feat")
    encoded = (hash_codes[0].astype(jnp.float32) * (2.0 / (BUCKETS - 1)) - 1.0).astype(jnp.bfloat16)
    first_pre = jnp.dot(encoded, encoder_first[0], preferred_element_type=jnp.float32)
    first_hidden = jax.nn.silu(first_pre).astype(jnp.bfloat16)
    row_table = jnp.dot(first_hidden, encoder_second[0], preferred_element_type=jnp.float32).astype(
        jnp.bfloat16
    )
    positions = sample_index[0]
    slot_count = row_table.shape[0]
    emb_width = row_table.shape[1]
    chunk_count = 2
    per_dest = positions.shape[0] // feat_count
    chunk_len = per_dest // chunk_count
    slot_iota = lax.broadcasted_iota(jnp.int32, (1, slot_count), 1)
    label_column = labels[:, 0]
    grad_parts = []
    for chunk in range(chunk_count):
        chunk_positions = positions.reshape(feat_count, per_dest)[
            :, chunk * chunk_len : (chunk + 1) * chunk_len
        ].reshape(-1)
        select = (chunk_positions[:, None] == slot_iota).astype(jnp.bfloat16)
        chosen_rows = (
            jnp.dot(select, row_table, preferred_element_type=jnp.float32)
            .astype(jnp.bfloat16)
            .reshape(feat_count, chunk_len, emb_width)
        )
        picked = lax.all_to_all(chosen_rows, "feat", split_axis=0, concat_axis=0, tiled=True)
        emb_delta = top_tower(
            picked,
            label_column[chunk * chunk_len : (chunk + 1) * chunk_len],
            top_weight,
            score_vector,
        )
        returned = lax.all_to_all(emb_delta, "feat", split_axis=0, concat_axis=0, tiled=True)
        grad_parts.append(
            jnp.einsum(
                "nu,ne->ue",
                select,
                returned.reshape(-1, emb_width),
                preferred_element_type=jnp.float32,
            )
        )
    row_grads = grad_parts[0]
    for part in grad_parts[1:]:
        row_grads = row_grads + part
    row_delta = row_grads.astype(jnp.bfloat16)
    second_local = jnp.einsum(
        "rk,re->ke", first_hidden, row_delta, preferred_element_type=jnp.float32
    )
    first_back = jnp.einsum(
        "re,ke->rk", row_delta, encoder_second[0], preferred_element_type=jnp.float32
    )
    first_delta = (first_back * silu_slope(first_pre)).astype(jnp.bfloat16)
    group_count = lax.axis_size("samp")
    shard_id = lax.axis_index("samp")
    hid_width = first_delta.shape[1]
    half_width = hid_width // 2
    first_rows = encoded.shape[1] // group_count
    second_rows = second_local.shape[0] // group_count
    second_split = second_local.astype(jnp.bfloat16).astype(jnp.float32).reshape(
        group_count, 2, second_rows // 2, emb_width
    )
    pieces = []
    for side in range(2):
        first_half = jnp.einsum(
            "rh,rk->hk",
            encoded,
            first_delta[:, side * half_width : (side + 1) * half_width],
            preferred_element_type=jnp.float32,
        )
        first_half = first_half.astype(jnp.bfloat16).astype(jnp.float32)
        pieces.append(
            jnp.concatenate(
                [first_half.reshape(group_count, first_rows, half_width), second_split[:, side]],
                axis=2,
            )
        )
    half_ring = group_count // 2
    plus_ring = [(j, (j + 1) % group_count) for j in range(group_count)]
    minus_ring = [(j, (j - 1) % group_count) for j in range(group_count)]
    plus_accs = [
        lax.dynamic_index_in_dim(piece, (shard_id + half_ring) % group_count, 0, keepdims=False)
        for piece in pieces
    ]
    minus_accs = [
        lax.dynamic_index_in_dim(
            piece, (shard_id - half_ring + 1) % group_count, 0, keepdims=False
        )
        for piece in pieces
    ]
    for hop in range(half_ring):
        for index, piece in enumerate(pieces):
            recv = lax.ppermute(plus_accs[index].astype(jnp.bfloat16), "samp", plus_ring)
            if hop < half_ring - 1:
                block = (shard_id + half_ring - 1 - hop) % group_count
                plus_accs[index] = recv.astype(jnp.float32) + lax.dynamic_index_in_dim(
                    piece, block, 0, keepdims=False
                )
            else:
                plus_accs[index] = recv.astype(jnp.float32)
            if hop < half_ring - 1:
                recv = lax.ppermute(minus_accs[index].astype(jnp.bfloat16), "samp", minus_ring)
                if hop < half_ring - 2:
                    block = (shard_id - half_ring + 2 + hop) % group_count
                    minus_accs[index] = recv.astype(jnp.float32) + lax.dynamic_index_in_dim(
                        piece, block, 0, keepdims=False
                    )
                else:
                    minus_accs[index] = recv.astype(jnp.float32)
    results = [
        plus_accs[index]
        + minus_accs[index]
        + lax.dynamic_index_in_dim(piece, shard_id, 0, keepdims=False)
        for index, piece in enumerate(pieces)
    ]
    share_first = jnp.concatenate([part[:, :half_width] for part in results], axis=1)
    share_second = jnp.concatenate([part[:, half_width:] for part in results], axis=0)
    return (row_grads[None], share_first[None], share_second[None])


def solution(mesh):
    return jax.shard_map(
        local,
        mesh=mesh,
        in_specs=(
            P("feat", "samp", None),
            P("feat", "samp"),
            P("feat", "samp"),
            P("feat", None, None),
            P("feat", None, None),
            P(),
            P(),
        ),
        out_specs=(P("feat", "samp", None), P("feat", "samp", None), P("feat", "samp", None)),
        check_vma=False,
    )
```

```python
import jax
import jax.numpy as jnp
from jax import lax
from jax.sharding import PartitionSpec as P

BUCKETS = 4096


loss_scale = 256.0


def silu_slope(inputs):
    logistic = jax.nn.sigmoid(inputs)
    return logistic * (1.0 + inputs * (1.0 - logistic))


def top_tower(picked, label_block, top_weight, score_vector):
    feats, count, width = picked.shape
    pair_dots = (
        jnp.einsum("fne,hne->nfh", picked, picked, preferred_element_type=jnp.float32)
        * width ** (-0.5)
    ).astype(jnp.bfloat16)
    pair_flat = pair_dots.reshape(count, feats * feats)
    top_pre = jnp.dot(pair_flat, top_weight, preferred_element_type=jnp.float32)
    top_hidden = jax.nn.silu(top_pre).astype(jnp.bfloat16)
    logits = jnp.dot(top_hidden, score_vector, preferred_element_type=jnp.float32)
    dlogit = loss_scale * (jax.nn.sigmoid(logits) - label_block.astype(jnp.float32))
    top_delta = (
        dlogit[:, None] * score_vector.astype(jnp.float32)[None, :] * silu_slope(top_pre)
    ).astype(jnp.bfloat16)
    pair_delta = jnp.einsum(
        "nk,jk->nj", top_delta, top_weight, preferred_element_type=jnp.float32
    ).reshape(count, feats, feats)
    pair_sym = (pair_delta + jnp.swapaxes(pair_delta, 1, 2)).astype(jnp.bfloat16)
    emb_delta = jnp.einsum(
        "nfh,hne->fne", pair_sym, picked, preferred_element_type=jnp.float32
    ) * width ** (-0.5)
    return emb_delta.astype(jnp.bfloat16)


def local(
    hash_codes, sample_index, labels, encoder_first, encoder_second, top_weight, score_vector
):
    feat_count = lax.axis_size("feat")
    encoded = (hash_codes[0].astype(jnp.float32) * (2.0 / (BUCKETS - 1)) - 1.0).astype(jnp.bfloat16)
    first_pre = jnp.dot(encoded, encoder_first[0], preferred_element_type=jnp.float32)
    first_hidden = jax.nn.silu(first_pre).astype(jnp.bfloat16)
    row_table = jnp.dot(first_hidden, encoder_second[0], preferred_element_type=jnp.float32).astype(
        jnp.bfloat16
    )
    positions = sample_index[0]
    slot_count = row_table.shape[0]
    emb_width = row_table.shape[1]
    chunk_count = 2
    per_dest = positions.shape[0] // feat_count
    chunk_len = per_dest // chunk_count
    slot_iota = lax.broadcasted_iota(jnp.int32, (1, slot_count), 1)
    label_column = labels[:, 0]
    grad_parts = []
    for chunk in range(chunk_count):
        chunk_positions = positions.reshape(feat_count, per_dest)[
            :, chunk * chunk_len : (chunk + 1) * chunk_len
        ].reshape(-1)
        select = (chunk_positions[:, None] == slot_iota).astype(jnp.bfloat16)
        chosen_rows = (
            jnp.dot(select, row_table, preferred_element_type=jnp.float32)
            .astype(jnp.bfloat16)
            .reshape(feat_count, chunk_len, emb_width)
        )
        picked = lax.all_to_all(chosen_rows, "feat", split_axis=0, concat_axis=0, tiled=True)
        emb_delta = top_tower(
            picked,
            label_column[chunk * chunk_len : (chunk + 1) * chunk_len],
            top_weight,
            score_vector,
        )
        returned = lax.all_to_all(emb_delta, "feat", split_axis=0, concat_axis=0, tiled=True)
        grad_parts.append(
            jnp.einsum(
                "nu,ne->ue",
                select,
                returned.reshape(-1, emb_width),
                preferred_element_type=jnp.float32,
            )
        )
    row_grads = grad_parts[0]
    for part in grad_parts[1:]:
        row_grads = row_grads + part
    row_delta = row_grads.astype(jnp.bfloat16)
    second_local = jnp.einsum(
        "rk,re->ke", first_hidden, row_delta, preferred_element_type=jnp.float32
    )
    first_back = jnp.einsum(
        "re,ke->rk", row_delta, encoder_second[0], preferred_element_type=jnp.float32
    )
    first_delta = (first_back * silu_slope(first_pre)).astype(jnp.bfloat16)
    group_count = lax.axis_size("samp")
    shard_id = lax.axis_index("samp")
    hid_width = first_delta.shape[1]
    half_width = hid_width // 2
    first_rows = encoded.shape[1] // group_count
    second_rows = second_local.shape[0] // group_count
    second_split = second_local.astype(jnp.bfloat16).astype(jnp.float32).reshape(
        group_count, 2, second_rows // 2, emb_width
    )
    pieces = []
    for side in range(2):
        first_half = jnp.einsum(
            "rh,rk->hk",
            encoded,
            first_delta[:, side * half_width : (side + 1) * half_width],
            preferred_element_type=jnp.float32,
        )
        first_half = first_half.astype(jnp.bfloat16).astype(jnp.float32)
        pieces.append(
            jnp.concatenate(
                [first_half.reshape(group_count, first_rows, half_width), second_split[:, side]],
                axis=2,
            )
        )
    half_ring = group_count // 2
    plus_ring = [(j, (j + 1) % group_count) for j in range(group_count)]
    minus_ring = [(j, (j - 1) % group_count) for j in range(group_count)]
    plus_accs = [
        lax.dynamic_index_in_dim(piece, (shard_id + half_ring) % group_count, 0, keepdims=False)
        for piece in pieces
    ]
    minus_accs = [
        lax.dynamic_index_in_dim(
            piece, (shard_id - half_ring + 1) % group_count, 0, keepdims=False
        )
        for piece in pieces
    ]
    for hop in range(half_ring):
        for index, piece in enumerate(pieces):
            recv = lax.ppermute(plus_accs[index].astype(jnp.bfloat16), "samp", plus_ring)
            if hop < half_ring - 1:
                block = (shard_id + half_ring - 1 - hop) % group_count
                plus_accs[index] = recv.astype(jnp.float32) + lax.dynamic_index_in_dim(
                    piece, block, 0, keepdims=False
                )
            else:
                plus_accs[index] = recv.astype(jnp.float32)
            if hop < half_ring - 1:
                recv = lax.ppermute(minus_accs[index].astype(jnp.bfloat16), "samp", minus_ring)
                if hop < half_ring - 2:
                    block = (shard_id - half_ring + 2 + hop) % group_count
                    minus_accs[index] = recv.astype(jnp.float32) + lax.dynamic_index_in_dim(
                        piece, block, 0, keepdims=False
                    )
                else:
                    minus_accs[index] = recv.astype(jnp.float32)
        tied = lax.optimization_barrier(tuple(plus_accs) + tuple(minus_accs))
        plus_accs = list(tied[: len(pieces)])
        minus_accs = list(tied[len(pieces) :])
    results = [
        plus_accs[index]
        + minus_accs[index]
        + lax.dynamic_index_in_dim(piece, shard_id, 0, keepdims=False)
        for index, piece in enumerate(pieces)
    ]
    share_first = jnp.concatenate([part[:, :half_width] for part in results], axis=1)
    share_second = jnp.concatenate([part[:, half_width:] for part in results], axis=0)
    return (row_grads[None], share_first[None], share_second[None])


def solution(mesh):
    return jax.shard_map(
        local,
        mesh=mesh,
        in_specs=(
            P("feat", "samp", None),
            P("feat", "samp"),
            P("feat", "samp"),
            P("feat", None, None),
            P("feat", None, None),
            P(),
            P(),
        ),
        out_specs=(P("feat", "samp", None), P("feat", "samp", None), P("feat", "samp", None)),
        check_vma=False,
    )
```

```python
import jax
import jax.numpy as jnp
from jax import lax
from jax.sharding import PartitionSpec as P

BUCKETS = 4096


loss_scale = 256.0


def silu_slope(inputs):
    logistic = jax.nn.sigmoid(inputs)
    return logistic * (1.0 + inputs * (1.0 - logistic))


def top_tower(picked, label_block, top_weight, score_vector):
    feats, count, width = picked.shape
    pair_dots = (
        jnp.einsum("fne,hne->nfh", picked, picked, preferred_element_type=jnp.float32)
        * width ** (-0.5)
    ).astype(jnp.bfloat16)
    pair_flat = pair_dots.reshape(count, feats * feats)
    top_pre = jnp.dot(pair_flat, top_weight, preferred_element_type=jnp.float32)
    top_hidden = jax.nn.silu(top_pre).astype(jnp.bfloat16)
    logits = jnp.dot(top_hidden, score_vector, preferred_element_type=jnp.float32)
    dlogit = loss_scale * (jax.nn.sigmoid(logits) - label_block.astype(jnp.float32))
    top_delta = (
        dlogit[:, None] * score_vector.astype(jnp.float32)[None, :] * silu_slope(top_pre)
    ).astype(jnp.bfloat16)
    pair_delta = jnp.einsum(
        "nk,jk->nj", top_delta, top_weight, preferred_element_type=jnp.float32
    ).reshape(count, feats, feats)
    pair_sym = (pair_delta + jnp.swapaxes(pair_delta, 1, 2)).astype(jnp.bfloat16)
    emb_delta = jnp.einsum(
        "nfh,hne->fne", pair_sym, picked, preferred_element_type=jnp.float32
    ) * width ** (-0.5)
    return emb_delta.astype(jnp.bfloat16)


def local(
    hash_codes, sample_index, labels, encoder_first, encoder_second, top_weight, score_vector
):
    feat_count = lax.axis_size("feat")
    encoded = (hash_codes[0].astype(jnp.float32) * (2.0 / (BUCKETS - 1)) - 1.0).astype(jnp.bfloat16)
    first_pre = jnp.dot(encoded, encoder_first[0], preferred_element_type=jnp.float32)
    first_pre = lax.optimization_barrier(first_pre)
    first_hidden = jax.nn.silu(first_pre).astype(jnp.bfloat16)
    row_table = jnp.dot(first_hidden, encoder_second[0], preferred_element_type=jnp.float32).astype(
        jnp.bfloat16
    )
    positions = sample_index[0]
    slot_count = row_table.shape[0]
    emb_width = row_table.shape[1]
    chunk_count = 2
    per_dest = positions.shape[0] // feat_count
    chunk_len = per_dest // chunk_count
    slot_iota = lax.broadcasted_iota(jnp.int32, (1, slot_count), 1)
    label_column = labels[:, 0]
    grad_parts = []
    for chunk in range(chunk_count):
        chunk_positions = positions.reshape(feat_count, per_dest)[
            :, chunk * chunk_len : (chunk + 1) * chunk_len
        ].reshape(-1)
        select = (chunk_positions[:, None] == slot_iota).astype(jnp.bfloat16)
        chosen_rows = (
            jnp.dot(select, row_table, preferred_element_type=jnp.float32)
            .astype(jnp.bfloat16)
            .reshape(feat_count, chunk_len, emb_width)
        )
        picked = lax.all_to_all(chosen_rows, "feat", split_axis=0, concat_axis=0, tiled=True)
        emb_delta = top_tower(
            picked,
            label_column[chunk * chunk_len : (chunk + 1) * chunk_len],
            top_weight,
            score_vector,
        )
        returned = lax.all_to_all(emb_delta, "feat", split_axis=0, concat_axis=0, tiled=True)
        grad_parts.append(
            jnp.einsum(
                "nu,ne->ue",
                select,
                returned.reshape(-1, emb_width),
                preferred_element_type=jnp.float32,
            )
        )
    row_grads = grad_parts[0]
    for part in grad_parts[1:]:
        row_grads = row_grads + part
    row_delta = row_grads.astype(jnp.bfloat16)
    second_local = jnp.einsum(
        "rk,re->ke", first_hidden, row_delta, preferred_element_type=jnp.float32
    )
    first_back = jnp.einsum(
        "re,ke->rk", row_delta, encoder_second[0], preferred_element_type=jnp.float32
    )
    first_delta = (first_back * silu_slope(first_pre)).astype(jnp.bfloat16)
    group_count = lax.axis_size("samp")
    shard_id = lax.axis_index("samp")
    hid_width = first_delta.shape[1]
    half_width = hid_width // 2
    first_rows = encoded.shape[1] // group_count
    second_rows = second_local.shape[0] // group_count
    second_split = second_local.astype(jnp.bfloat16).astype(jnp.float32).reshape(
        group_count, 2, second_rows // 2, emb_width
    )
    pieces = []
    for side in range(2):
        first_half = jnp.einsum(
            "rh,rk->hk",
            encoded,
            first_delta[:, side * half_width : (side + 1) * half_width],
            preferred_element_type=jnp.float32,
        )
        first_half = first_half.astype(jnp.bfloat16).astype(jnp.float32)
        pieces.append(
            jnp.concatenate(
                [first_half.reshape(group_count, first_rows, half_width), second_split[:, side]],
                axis=2,
            )
        )
    chains = []
    for side, step in ((0, 1), (1, -1)):
        piece_rows = pieces[side].shape[1] // 2
        for part in range(2):
            piece = pieces[side][:, part * piece_rows : (part + 1) * piece_rows]
            acc = lax.dynamic_index_in_dim(
                piece, (shard_id - step) % group_count, 0, keepdims=False
            )
            chains.append([piece, step, acc])
    for hop in range(group_count - 1):
        for chain in chains:
            piece, step, acc = chain
            ring = [(j, (j + step) % group_count) for j in range(group_count)]
            recv = lax.ppermute(acc.astype(jnp.bfloat16), "samp", ring)
            block = (shard_id - step * (hop + 2)) % group_count
            chain[2] = recv.astype(jnp.float32) + lax.dynamic_index_in_dim(
                piece, block, 0, keepdims=False
            )
    results = [
        jnp.concatenate([chains[0][2], chains[1][2]], axis=0),
        jnp.concatenate([chains[2][2], chains[3][2]], axis=0),
    ]
    share_first = jnp.concatenate([part[:, :half_width] for part in results], axis=1)
    share_second = jnp.concatenate([part[:, half_width:] for part in results], axis=0)
    return (row_grads[None], share_first[None], share_second[None])


def solution(mesh):
    return jax.shard_map(
        local,
        mesh=mesh,
        in_specs=(
            P("feat", "samp", None),
            P("feat", "samp"),
            P("feat", "samp"),
            P("feat", None, None),
            P("feat", None, None),
            P(),
            P(),
        ),
        out_specs=(P("feat", "samp", None), P("feat", "samp", None), P("feat", "samp", None)),
        check_vma=False,
    )
```

```python
import jax
import jax.numpy as jnp
from jax import lax
from jax.sharding import PartitionSpec as P

BUCKETS = 4096


loss_scale = 256.0


def silu_slope(inputs):
    logistic = jax.nn.sigmoid(inputs)
    return logistic * (1.0 + inputs * (1.0 - logistic))


def top_tower(picked, label_block, top_weight, score_vector):
    feats, count, width = picked.shape
    pair_dots = (
        jnp.einsum("fne,hne->nfh", picked, picked, preferred_element_type=jnp.float32)
        * width ** (-0.5)
    ).astype(jnp.bfloat16)
    pair_flat = pair_dots.reshape(count, feats * feats)
    top_pre = jnp.dot(pair_flat, top_weight, preferred_element_type=jnp.float32)
    top_hidden = jax.nn.silu(top_pre).astype(jnp.bfloat16)
    logits = jnp.dot(top_hidden, score_vector, preferred_element_type=jnp.float32)
    dlogit = loss_scale * (jax.nn.sigmoid(logits) - label_block.astype(jnp.float32))
    top_delta = (
        dlogit[:, None] * score_vector.astype(jnp.float32)[None, :] * silu_slope(top_pre)
    ).astype(jnp.bfloat16)
    pair_delta = jnp.einsum(
        "nk,jk->nj", top_delta, top_weight, preferred_element_type=jnp.float32
    ).reshape(count, feats, feats)
    pair_sym = (pair_delta + jnp.swapaxes(pair_delta, 1, 2)).astype(jnp.bfloat16)
    emb_delta = jnp.einsum(
        "nfh,hne->fne", pair_sym, picked, preferred_element_type=jnp.float32
    ) * width ** (-0.5)
    return emb_delta.astype(jnp.bfloat16)


def local(
    hash_codes, sample_index, labels, encoder_first, encoder_second, top_weight, score_vector
):
    feat_count = lax.axis_size("feat")
    encoded = (hash_codes[0].astype(jnp.float32) * (2.0 / (BUCKETS - 1)) - 1.0).astype(jnp.bfloat16)
    first_pre = jnp.dot(encoded, encoder_first[0], preferred_element_type=jnp.float32)
    first_hidden = jax.nn.silu(first_pre).astype(jnp.bfloat16)
    row_table = jnp.dot(first_hidden, encoder_second[0], preferred_element_type=jnp.float32).astype(
        jnp.bfloat16
    )
    positions = sample_index[0]
    slot_count = row_table.shape[0]
    emb_width = row_table.shape[1]
    chunk_count = 2
    per_dest = positions.shape[0] // feat_count
    chunk_len = per_dest // chunk_count
    slot_iota = lax.broadcasted_iota(jnp.int32, (1, slot_count), 1)
    label_column = labels[:, 0]
    grad_parts = []
    for chunk in range(chunk_count):
        chunk_positions = positions.reshape(feat_count, per_dest)[
            :, chunk * chunk_len : (chunk + 1) * chunk_len
        ].reshape(-1)
        select = (chunk_positions[:, None] == slot_iota).astype(jnp.bfloat16)
        chosen_rows = (
            jnp.dot(select, row_table, preferred_element_type=jnp.float32)
            .astype(jnp.bfloat16)
            .reshape(feat_count, chunk_len, emb_width)
        )
        picked = lax.all_to_all(chosen_rows, "feat", split_axis=0, concat_axis=0, tiled=True)
        emb_delta = top_tower(
            picked,
            label_column[chunk * chunk_len : (chunk + 1) * chunk_len],
            top_weight,
            score_vector,
        )
        returned = lax.all_to_all(emb_delta, "feat", split_axis=0, concat_axis=0, tiled=True)
        grad_parts.append(
            jnp.einsum(
                "nu,ne->ue",
                select,
                returned.reshape(-1, emb_width),
                preferred_element_type=jnp.float32,
            )
        )
    row_grads = grad_parts[0]
    for part in grad_parts[1:]:
        row_grads = row_grads + part
    row_delta = row_grads.astype(jnp.bfloat16)
    second_local = jnp.einsum(
        "rk,re->ke", first_hidden, row_delta, preferred_element_type=jnp.float32
    )
    first_back = jnp.einsum(
        "re,ke->rk", row_delta, encoder_second[0], preferred_element_type=jnp.float32
    )
    first_delta = (first_back * silu_slope(first_pre)).astype(jnp.bfloat16)
    group_count = lax.axis_size("samp")
    shard_id = lax.axis_index("samp")
    hid_width = first_delta.shape[1]
    half_width = hid_width // 2
    first_rows = encoded.shape[1] // group_count
    second_rows = second_local.shape[0] // group_count
    second_split = second_local.astype(jnp.bfloat16).reshape(
        group_count, 2, second_rows // 2, emb_width
    )
    pieces = []
    for side in range(2):
        first_half = jnp.einsum(
            "rh,rk->hk",
            encoded,
            first_delta[:, side * half_width : (side + 1) * half_width],
            preferred_element_type=jnp.float32,
        )
        first_half = first_half.astype(jnp.bfloat16)
        pieces.append(
            jnp.concatenate(
                [first_half.reshape(group_count, first_rows, half_width), second_split[:, side]],
                axis=2,
            )
        )
    chains = []
    for side, step in ((0, 1), (1, -1)):
        piece_rows = pieces[side].shape[1] // 2
        for part in range(2):
            piece = pieces[side][:, part * piece_rows : (part + 1) * piece_rows]
            acc = lax.dynamic_index_in_dim(
                piece, (shard_id - step) % group_count, 0, keepdims=False
            ).astype(jnp.float32)
            chains.append([piece, step, acc])
    for hop in range(group_count - 1):
        for chain in chains:
            piece, step, acc = chain
            ring = [(j, (j + step) % group_count) for j in range(group_count)]
            recv = lax.ppermute(acc.astype(jnp.bfloat16), "samp", ring)
            block = (shard_id - step * (hop + 2)) % group_count
            chain[2] = recv.astype(jnp.float32) + lax.dynamic_index_in_dim(
                piece, block, 0, keepdims=False
            ).astype(jnp.float32)
    results = [
        jnp.concatenate([chains[0][2], chains[1][2]], axis=0),
        jnp.concatenate([chains[2][2], chains[3][2]], axis=0),
    ]
    share_first = jnp.concatenate([part[:, :half_width] for part in results], axis=1)
    share_second = jnp.concatenate([part[:, half_width:] for part in results], axis=0)
    return (row_grads[None], share_first[None], share_second[None])


def solution(mesh):
    return jax.shard_map(
        local,
        mesh=mesh,
        in_specs=(
            P("feat", "samp", None),
            P("feat", "samp"),
            P("feat", "samp"),
            P("feat", None, None),
            P("feat", None, None),
            P(),
            P(),
        ),
        out_specs=(P("feat", "samp", None), P("feat", "samp", None), P("feat", "samp", None)),
        check_vma=False,
    )
```

```python
import jax
import jax.numpy as jnp
from jax import lax
from jax.sharding import PartitionSpec as P

BUCKETS = 4096


loss_scale = 256.0


def silu_slope(inputs):
    logistic = jax.nn.sigmoid(inputs)
    return logistic * (1.0 + inputs * (1.0 - logistic))


def top_tower(picked, label_block, top_weight, score_vector):
    feats, count, width = picked.shape
    pair_dots = (
        jnp.einsum("fne,hne->nfh", picked, picked, preferred_element_type=jnp.float32)
        * width ** (-0.5)
    ).astype(jnp.bfloat16)
    pair_flat = pair_dots.reshape(count, feats * feats)
    top_pre = jnp.dot(pair_flat, top_weight, preferred_element_type=jnp.float32)
    top_hidden = jax.nn.silu(top_pre).astype(jnp.bfloat16)
    logits = jnp.dot(top_hidden, score_vector, preferred_element_type=jnp.float32)
    dlogit = loss_scale * (jax.nn.sigmoid(logits) - label_block.astype(jnp.float32))
    top_delta = (
        dlogit[:, None] * score_vector.astype(jnp.float32)[None, :] * silu_slope(top_pre)
    ).astype(jnp.bfloat16)
    pair_delta = jnp.einsum(
        "nk,jk->nj", top_delta, top_weight, preferred_element_type=jnp.float32
    ).reshape(count, feats, feats)
    pair_sym = (pair_delta + jnp.swapaxes(pair_delta, 1, 2)).astype(jnp.bfloat16)
    emb_delta = jnp.einsum(
        "nfh,hne->fne", pair_sym, picked, preferred_element_type=jnp.float32
    ) * width ** (-0.5)
    return emb_delta.astype(jnp.bfloat16)


def local(
    hash_codes, sample_index, labels, encoder_first, encoder_second, top_weight, score_vector
):
    feat_count = lax.axis_size("feat")
    encoded = (hash_codes[0].astype(jnp.float32) * (2.0 / (BUCKETS - 1)) - 1.0).astype(jnp.bfloat16)
    first_pre = jnp.dot(encoded, encoder_first[0], preferred_element_type=jnp.float32)
    first_hidden = jax.nn.silu(first_pre).astype(jnp.bfloat16)
    kept_pre = first_pre.astype(jnp.bfloat16)
    row_table = jnp.dot(first_hidden, encoder_second[0], preferred_element_type=jnp.float32).astype(
        jnp.bfloat16
    )
    positions = sample_index[0]
    slot_count = row_table.shape[0]
    emb_width = row_table.shape[1]
    chunk_count = 2
    per_dest = positions.shape[0] // feat_count
    chunk_len = per_dest // chunk_count
    slot_iota = lax.broadcasted_iota(jnp.int32, (1, slot_count), 1)
    label_column = labels[:, 0]
    grad_parts = []
    for chunk in range(chunk_count):
        chunk_positions = positions.reshape(feat_count, per_dest)[
            :, chunk * chunk_len : (chunk + 1) * chunk_len
        ].reshape(-1)
        select = (chunk_positions[:, None] == slot_iota).astype(jnp.bfloat16)
        chosen_rows = (
            jnp.dot(select, row_table, preferred_element_type=jnp.float32)
            .astype(jnp.bfloat16)
            .reshape(feat_count, chunk_len, emb_width)
        )
        picked = lax.all_to_all(chosen_rows, "feat", split_axis=0, concat_axis=0, tiled=True)
        emb_delta = top_tower(
            picked,
            label_column[chunk * chunk_len : (chunk + 1) * chunk_len],
            top_weight,
            score_vector,
        )
        returned = lax.all_to_all(emb_delta, "feat", split_axis=0, concat_axis=0, tiled=True)
        grad_parts.append(
            jnp.einsum(
                "nu,ne->ue",
                select,
                returned.reshape(-1, emb_width),
                preferred_element_type=jnp.float32,
            )
        )
    row_grads = grad_parts[0]
    for part in grad_parts[1:]:
        row_grads = row_grads + part
    row_delta = row_grads.astype(jnp.bfloat16)
    second_local = jnp.einsum(
        "rk,re->ke", first_hidden, row_delta, preferred_element_type=jnp.float32
    )
    first_back = jnp.einsum(
        "re,ke->rk", row_delta, encoder_second[0], preferred_element_type=jnp.float32
    )
    first_delta = (first_back * silu_slope(kept_pre.astype(jnp.float32))).astype(jnp.bfloat16)
    group_count = lax.axis_size("samp")
    shard_id = lax.axis_index("samp")
    hid_width = first_delta.shape[1]
    half_width = hid_width // 2
    first_rows = encoded.shape[1] // group_count
    second_rows = second_local.shape[0] // group_count
    second_split = second_local.astype(jnp.bfloat16).reshape(
        group_count, 2, second_rows // 2, emb_width
    )
    pieces = []
    for side in range(2):
        first_half = jnp.einsum(
            "rh,rk->hk",
            encoded,
            first_delta[:, side * half_width : (side + 1) * half_width],
            preferred_element_type=jnp.float32,
        )
        first_half = first_half.astype(jnp.bfloat16)
        pieces.append(
            jnp.concatenate(
                [first_half.reshape(group_count, first_rows, half_width), second_split[:, side]],
                axis=2,
            )
        )
    chains = []
    for side, step in ((0, 1), (1, -1)):
        piece_rows = pieces[side].shape[1] // 2
        for part in range(2):
            piece = pieces[side][:, part * piece_rows : (part + 1) * piece_rows]
            acc = lax.dynamic_index_in_dim(
                piece, (shard_id - step) % group_count, 0, keepdims=False
            ).astype(jnp.float32)
            chains.append([piece, step, acc])
    for hop in range(group_count - 1):
        for chain in chains:
            piece, step, acc = chain
            ring = [(j, (j + step) % group_count) for j in range(group_count)]
            recv = lax.ppermute(acc.astype(jnp.bfloat16), "samp", ring)
            block = (shard_id - step * (hop + 2)) % group_count
            chain[2] = recv.astype(jnp.float32) + lax.dynamic_index_in_dim(
                piece, block, 0, keepdims=False
            ).astype(jnp.float32)
    results = [
        jnp.concatenate([chains[0][2], chains[1][2]], axis=0),
        jnp.concatenate([chains[2][2], chains[3][2]], axis=0),
    ]
    share_first = jnp.concatenate([part[:, :half_width] for part in results], axis=1)
    share_second = jnp.concatenate([part[:, half_width:] for part in results], axis=0)
    return (row_grads[None], share_first[None], share_second[None])


def solution(mesh):
    return jax.shard_map(
        local,
        mesh=mesh,
        in_specs=(
            P("feat", "samp", None),
            P("feat", "samp"),
            P("feat", "samp"),
            P("feat", None, None),
            P("feat", None, None),
            P(),
            P(),
        ),
        out_specs=(P("feat", "samp", None), P("feat", "samp", None), P("feat", "samp", None)),
        check_vma=False,
    )
```
